32 devices in a mesh: src: 4 (over x, core), ep: 8 (over z, y).
Axes of the slice: x: 2, y: 2, z: 4, core: 2. Of those that a mesh axis runs over, the one named last changes fastest.
Arguments:
- log_conductivity: float32 [8, 16, 32, 128], P('ep'), may hold values from -3 to 3
- forward_field: float32 [8, 4, 16, 32, 128], P('ep', 'src'), may hold values from -6 to 6
- adjoint_field: float32 [8, 4, 16, 32, 128], P('ep', 'src'), may hold values from -6 to 6
- source_cells: int32 [4, 2], P('src'), may hold values from 0 to 65535
- receiver_cells: int32 [128], replicated, may hold values from 0 to 65535
- observed: float32 [8, 4, 128], P('ep', 'src'), may hold values from -6 to 6
- split_term: float32 [6, 65536], P(None, ('src', 'ep')), may hold values from -1.2 to 1.2
- dual_term: float32 [6, 65536], P(None, ('src', 'ep')), may hold values from -1.2 to 1.2
Outputs:
- model_out: float32 [8, 16, 32, 128], P('ep')
- split_out: float32 [6, 65536], P(None, ('src', 'ep'))
- dual_out: float32 [6, 65536], P(None, ('src', 'ep'))
The draws below stay inside these ranges and needn't reach their ends.
Inputs may be any that keep to these rules, and one draw needn't show every extreme that they name: `source_cells`: source and receiver cells may repeat; a source's two electrodes may coincide.
All inputs are finite; a program needn't handle non-finite values.
Results may differ from the reference program's by a relative error of at most 0.0003.
Values sent between devices are 32-bit elements; how exact they have to be, the bound alone decides.
No kernel may reach another device: no remote copies, remote signals or barrier semaphores. Data moves between devices by JAX's collectives and lax.ppermute only.
A program may use at most 128 MiB of HBM per device.

```python
import jax
import jax.numpy as jnp
from jax import lax

GX = 16
GY = 32
GZ = 128
RECEIVERS = 128
SWEEPS = 4
ITERS = 1
CELLS = 65536
SOURCES = 4
EPOCHS = 8


def place_ends(entries, rng, smallest, top_value):
    spot = [jax.random.randint(jax.random.fold_in(rng, axis), (), 0, length) for axis, length in enumerate(entries.shape)]
    widest = entries.shape.index(max(entries.shape))
    neighbour = spot[:widest] + [(spot[widest] + 1) % entries.shape[widest]] + spot[widest + 1:]
    return entries.at[tuple(spot)].set(smallest).at[tuple(neighbour)].set(top_value)


def steps_of(key, shape, pieces, least, largest):
    gain = 1.0
    for dim, parts in pieces:
        steps = jax.random.uniform(jax.random.fold_in(jax.random.fold_in(key, 6), dim), (parts,), jnp.float32, least / len(pieces), largest / len(pieces))
        gain = gain * jnp.repeat(jnp.exp(steps), shape[dim] // parts).reshape((-1,) + (1,) * (len(shape) - 1 - dim))
    return gain


def scatter_about(stream_key, shape, deviation, most, pieces=(), held_as=jnp.bfloat16):
    gain = steps_of(stream_key, shape, pieces, -0.22, 0.18) if pieces else 1.0
    drawn = jax.random.normal(stream_key, shape, jnp.float32) * deviation * gain
    return jnp.minimum(jnp.maximum(drawn, -most), most).astype(held_as)


def setup_inputs(seed: int = 0) -> dict:
    splits = jax.random.split(jax.random.key(seed), 9)
    log_conductivity = scatter_about(splits[0], (EPOCHS, GX, GY, GZ), 0.5, 3.0, ((0, 8),), jnp.float32)
    forward_field = scatter_about(splits[1], (EPOCHS, SOURCES, GX, GY, GZ), 1.0, 6.0, ((0, 8), (1, 4)), jnp.float32)
    adjoint_field = scatter_about(splits[2], (EPOCHS, SOURCES, GX, GY, GZ), 1.0, 6.0, ((0, 8), (1, 4)), jnp.float32)
    source_cells = place_ends(jax.random.randint(splits[3], (SOURCES, 2), 0, CELLS), jax.random.fold_in(splits[3], 1), 0, CELLS - 1).astype(jnp.int32)
    receiver_cells = place_ends(jax.random.randint(splits[4], (RECEIVERS,), 0, CELLS), jax.random.fold_in(splits[4], 1), 0, CELLS - 1).astype(jnp.int32)
    observed = scatter_about(splits[5], (EPOCHS, SOURCES, RECEIVERS), 1.0, 6.0, ((0, 8), (1, 4)), jnp.float32)
    split_term = scatter_about(splits[6], (EPOCHS - 2, CELLS), 0.2, 1.2, ((1, 32),), jnp.float32)
    dual_term = scatter_about(splits[7], (EPOCHS - 2, CELLS), 0.2, 1.2, ((1, 32),), jnp.float32)
    return {"log_conductivity": log_conductivity, "forward_field": forward_field, "adjoint_field": adjoint_field, "source_cells": source_cells, "receiver_cells": receiver_cells, "observed": observed, "split_term": split_term, "dual_term": dual_term}


MASS_TERM = 0.5
RELAXATION = 0.8
CURRENT = 4.0
DATA_WEIGHT = 8.0
STEP_SIZE = 0.5
PENALTY = 64.0
THRESHOLD = 0.1

def pad_side(values, dim_index, at_low):
    widths = [(0, 0)] * values.ndim
    widths[dim_index] = (0, 1) if at_low else (1, 0)
    return jnp.pad(values, widths)

def conductances(conductivity):
    face_weights = []
    diagonal = MASS_TERM * conductivity
    ndims = conductivity.ndim
    for dim_index in range(ndims - 3, ndims):
        length = conductivity.shape[dim_index]
        lower_cells = lax.slice_in_dim(conductivity, 0, length - 1, axis=dim_index)
        upper_cells = lax.slice_in_dim(conductivity, 1, length, axis=dim_index)
        face_weight = 0.5 * (lower_cells + upper_cells)
        face_weights.append(face_weight)
        diagonal = diagonal + pad_side(face_weight, dim_index, True) + pad_side(face_weight, dim_index, False)
    return (face_weights, diagonal)

def operate(iterate, conductivity, face_weights):
    result = MASS_TERM * conductivity * iterate
    ndims = iterate.ndim
    for position, dim_index in enumerate(range(ndims - 3, ndims)):
        length = iterate.shape[dim_index]
        face_flux = face_weights[position] * (lax.slice_in_dim(iterate, 1, length, axis=dim_index) - lax.slice_in_dim(iterate, 0, length - 1, axis=dim_index))
        result = result - pad_side(face_flux, dim_index, True) + pad_side(face_flux, dim_index, False)
    return result

def relax(iterate, right_side, conductivity, face_weights, diagonal):
    for sweep_index in range(SWEEPS):
        iterate = iterate + RELAXATION * (right_side - operate(iterate, conductivity, face_weights)) / diagonal
    return iterate

def source_field(source_cells, cell_count):
    source_count = source_cells.shape[0]
    row_index = jnp.arange(source_count, dtype=jnp.int32)[:, None] * jnp.ones((1, 2), jnp.int32)
    polarity = jnp.broadcast_to(jnp.array([CURRENT, -CURRENT], jnp.float32), (source_count, 2))
    return jnp.zeros((source_count, cell_count), jnp.float32).at[row_index, source_cells.astype(jnp.int32)].add(polarity)

def sweep_epoch(model_log, forward, adjoint, sources, receiver_cells, observed):
    grid_shape = forward.shape
    conductivity = jnp.exp(model_log)[None]
    face_weights, diagonal = conductances(conductivity)
    forward = relax(forward, sources.reshape(grid_shape), conductivity, face_weights, diagonal)
    flat_field = forward.reshape(grid_shape[0], -1)
    misfit = flat_field[:, receiver_cells] - observed
    adjoint_source = jnp.zeros_like(flat_field).at[:, receiver_cells].add(DATA_WEIGHT * misfit).reshape(grid_shape)
    adjoint = relax(adjoint, adjoint_source, conductivity, face_weights, diagonal)
    gradient = conductivity[0] * jnp.sum(forward * adjoint, axis=0)
    return (forward, adjoint, gradient)

def temporal_factor(epochs):
    second = jnp.eye(epochs - 2, epochs, dtype=jnp.float32) - 2.0 * jnp.eye(epochs - 2, epochs, k=1, dtype=jnp.float32) + jnp.eye(epochs - 2, epochs, k=2, dtype=jnp.float32)
    matrix = jnp.eye(epochs, dtype=jnp.float32) + PENALTY * jnp.dot(second.T, second, precision=lax.Precision.HIGHEST)
    return jnp.linalg.cholesky(matrix)

def difference(values):
    return values[:-2] - 2.0 * values[1:-1] + values[2:]

def difference_adjoint(values):
    widths_low = [(0, 2), (0, 0)]
    widths_mid = [(1, 1), (0, 0)]
    widths_high = [(2, 0), (0, 0)]
    return jnp.pad(values, widths_low) - 2.0 * jnp.pad(values, widths_mid) + jnp.pad(values, widths_high)

def splitting_update(local_rhs, split_term, dual_term, factor):
    right_side = local_rhs + PENALTY * difference_adjoint(split_term - dual_term)
    updated = jax.scipy.linalg.cho_solve((factor, True), right_side)
    shifted = difference(updated) + dual_term
    split_term = shifted - jnp.clip(shifted, -THRESHOLD, THRESHOLD)
    dual_term = shifted - split_term
    return (updated, split_term, dual_term)

def reference(log_conductivity, forward_field, adjoint_field, source_cells, receiver_cells, observed, split_term, dual_term):
    sources = source_field(source_cells, CELLS)
    factor = temporal_factor(EPOCHS)
    model_log = log_conductivity
    forward = forward_field
    adjoint = adjoint_field
    receivers = receiver_cells.astype(jnp.int32)
    for round_index in range(ITERS):

        def per_epoch(epoch_items):
            return sweep_epoch(epoch_items[0], epoch_items[1], epoch_items[2], sources, receivers, epoch_items[3])
        forward, adjoint, gradient = lax.map(per_epoch, (model_log, forward, adjoint, observed))
        local_rhs = model_log.reshape(EPOCHS, CELLS) - STEP_SIZE * gradient.reshape(EPOCHS, CELLS)
        updated, split_term, dual_term = splitting_update(local_rhs, split_term, dual_term, factor)
        model_log = updated.reshape(log_conductivity.shape)
    return (model_log, split_term, dual_term)
```

```python
import jax
import jax.numpy as jnp
from jax import lax
from jax.sharding import PartitionSpec as P

SWEEPS = 4


MASS_TERM = 0.5
RELAXATION = 0.8
CURRENT = 4.0
DATA_WEIGHT = 8.0
STEP_SIZE = 0.5
PENALTY = 64.0
THRESHOLD = 0.1


def pad_side(values, dim_index, at_low):
    widths = [(0, 0)] * values.ndim
    widths[dim_index] = (0, 1) if at_low else (1, 0)
    return jnp.pad(values, widths)


def conductances(conductivity):
    face_weights = []
    diagonal = MASS_TERM * conductivity
    ndims = conductivity.ndim
    for dim_index in range(ndims - 3, ndims):
        length = conductivity.shape[dim_index]
        lower_cells = lax.slice_in_dim(conductivity, 0, length - 1, axis=dim_index)
        upper_cells = lax.slice_in_dim(conductivity, 1, length, axis=dim_index)
        face_weight = 0.5 * (lower_cells + upper_cells)
        face_weights.append(face_weight)
        diagonal = (
            diagonal
            + pad_side(face_weight, dim_index, True)
            + pad_side(face_weight, dim_index, False)
        )
    return (face_weights, diagonal)


def operate(iterate, conductivity, face_weights):
    result = MASS_TERM * conductivity * iterate
    ndims = iterate.ndim
    for position, dim_index in enumerate(range(ndims - 3, ndims)):
        length = iterate.shape[dim_index]
        face_flux = face_weights[position] * (
            lax.slice_in_dim(iterate, 1, length, axis=dim_index)
            - lax.slice_in_dim(iterate, 0, length - 1, axis=dim_index)
        )
        result = (
            result - pad_side(face_flux, dim_index, True) + pad_side(face_flux, dim_index, False)
        )
    return result


def relax(iterate, right_side, conductivity, face_weights, diagonal):
    for sweep_index in range(SWEEPS):
        iterate = (
            iterate
            + RELAXATION * (right_side - operate(iterate, conductivity, face_weights)) / diagonal
        )
    return iterate


def source_field(source_cells, cell_count):
    source_count = source_cells.shape[0]
    row_index = jnp.arange(source_count, dtype=jnp.int32)[:, None] * jnp.ones((1, 2), jnp.int32)
    polarity = jnp.broadcast_to(jnp.array([CURRENT, -CURRENT], jnp.float32), (source_count, 2))
    return (
        jnp.zeros((source_count, cell_count), jnp.float32).at[row_index, source_cells].add(polarity)
    )


def sweep_epoch(model_log, forward, adjoint, sources, receiver_cells, observed):
    grid_shape = forward.shape
    conductivity = jnp.exp(model_log)[None]
    face_weights, diagonal = conductances(conductivity)
    forward = relax(forward, sources.reshape(grid_shape), conductivity, face_weights, diagonal)
    flat_field = forward.reshape(grid_shape[0], -1)
    misfit = flat_field[:, receiver_cells] - observed
    adjoint_source = (
        jnp.zeros_like(flat_field)
        .at[:, receiver_cells]
        .add(DATA_WEIGHT * misfit)
        .reshape(grid_shape)
    )
    adjoint = relax(adjoint, adjoint_source, conductivity, face_weights, diagonal)
    gradient = conductivity[0] * jnp.sum(forward * adjoint, axis=0)
    return (forward, adjoint, gradient)


def temporal_factor(epochs):
    second = (
        jnp.eye(epochs - 2, epochs, dtype=jnp.float32)
        - 2.0 * jnp.eye(epochs - 2, epochs, k=1, dtype=jnp.float32)
        + jnp.eye(epochs - 2, epochs, k=2, dtype=jnp.float32)
    )
    matrix = jnp.eye(epochs, dtype=jnp.float32) + PENALTY * jnp.dot(
        second.T, second, precision=lax.Precision.HIGHEST
    )
    return jnp.linalg.cholesky(matrix)


def difference(values):
    return values[:-2] - 2.0 * values[1:-1] + values[2:]


def difference_adjoint(values):
    widths_low = [(0, 2), (0, 0)]
    widths_mid = [(1, 1), (0, 0)]
    widths_high = [(2, 0), (0, 0)]
    return (
        jnp.pad(values, widths_low)
        - 2.0 * jnp.pad(values, widths_mid)
        + jnp.pad(values, widths_high)
    )


def splitting_update(local_rhs, split_term, dual_term, factor):
    right_side = local_rhs + PENALTY * difference_adjoint(split_term - dual_term)
    updated = jax.scipy.linalg.cho_solve((factor, True), right_side)
    shifted = difference(updated) + dual_term
    split_term = shifted - jnp.clip(shifted, -THRESHOLD, THRESHOLD)
    dual_term = shifted - split_term
    return (updated, split_term, dual_term)


def on_device(
    log_conductivity,
    forward_field,
    adjoint_field,
    source_cells,
    receiver_cells,
    observed,
    split_term,
    dual_term,
):
    slab_epochs, size_x, size_y, size_z = log_conductivity.shape
    cell_count = size_x * size_y * size_z
    src_count = lax.axis_size("src")
    ep_count = lax.axis_size("ep")
    devices = src_count * ep_count
    share_cells = cell_count // devices
    total_epochs = slab_epochs * ep_count
    sources = source_field(source_cells, cell_count)
    factor = temporal_factor(total_epochs)
    sweeper = jax.vmap(sweep_epoch, in_axes=(0, 0, 0, None, None, 0))
    model_log = log_conductivity
    forward, adjoint, partial_terms = sweeper(
        model_log, forward_field, adjoint_field, sources, receiver_cells, observed
    )
    own_model = jnp.where(lax.axis_index("src") == 0, 1.0, 0.0) * model_log.reshape(
        slab_epochs, cell_count
    )
    partial_rhs = own_model - STEP_SIZE * partial_terms.reshape(slab_epochs, cell_count)
    sent = partial_rhs.reshape(slab_epochs, devices, share_cells).transpose(1, 0, 2)
    got = lax.all_to_all(sent, ("src", "ep"), split_axis=0, concat_axis=0, tiled=True)
    time_rhs = got.reshape(src_count, total_epochs, share_cells).sum(axis=0)
    updated, split_term, dual_term = splitting_update(time_rhs, split_term, dual_term, factor)
    back = jnp.broadcast_to(
        updated.reshape(1, ep_count, slab_epochs, share_cells),
        (src_count, ep_count, slab_epochs, share_cells),
    ).reshape(devices, slab_epochs, share_cells)
    model_rows = lax.all_to_all(back, ("src", "ep"), split_axis=0, concat_axis=0, tiled=True)
    model_log = model_rows.transpose(1, 0, 2).reshape(slab_epochs, size_x, size_y, size_z)
    return (model_log, split_term, dual_term)


def solution(mesh):
    return jax.shard_map(
        on_device,
        mesh=mesh,
        in_specs=(
            P("ep", None, None, None),
            P("ep", "src", None, None, None),
            P("ep", "src", None, None, None),
            P("src", None),
            P(),
            P("ep", "src", None),
            P(None, ("src", "ep")),
            P(None, ("src", "ep")),
        ),
        out_specs=(P("ep", None, None, None), P(None, ("src", "ep")), P(None, ("src", "ep"))),
        check_vma=False,
    )
```

```python
import functools

import jax
import jax.numpy as jnp
from jax import lax
from jax.sharding import PartitionSpec as P
from jax.experimental import pallas as pl
from jax.experimental.pallas import tpu as pltpu

SWEEPS = 4


MASS_TERM = 0.5
RELAXATION = 0.8
CURRENT = 4.0
DATA_WEIGHT = 8.0
STEP_SIZE = 0.5
PENALTY = 64.0
THRESHOLD = 0.1


def pad_side(values, dim_index, at_low):
    widths = [(0, 0)] * values.ndim
    widths[dim_index] = (0, 1) if at_low else (1, 0)
    return jnp.pad(values, widths)


def conductances(conductivity):
    face_weights = []
    diagonal = MASS_TERM * conductivity
    ndims = conductivity.ndim
    for dim_index in range(ndims - 3, ndims):
        length = conductivity.shape[dim_index]
        lower_cells = lax.slice_in_dim(conductivity, 0, length - 1, axis=dim_index)
        upper_cells = lax.slice_in_dim(conductivity, 1, length, axis=dim_index)
        face_weight = 0.5 * (lower_cells + upper_cells)
        face_weights.append(face_weight)
        diagonal = (
            diagonal
            + pad_side(face_weight, dim_index, True)
            + pad_side(face_weight, dim_index, False)
        )
    return (face_weights, diagonal)


def operate(iterate, conductivity, face_weights):
    result = MASS_TERM * conductivity * iterate
    ndims = iterate.ndim
    for position, dim_index in enumerate(range(ndims - 3, ndims)):
        length = iterate.shape[dim_index]
        face_flux = face_weights[position] * (
            lax.slice_in_dim(iterate, 1, length, axis=dim_index)
            - lax.slice_in_dim(iterate, 0, length - 1, axis=dim_index)
        )
        result = (
            result - pad_side(face_flux, dim_index, True) + pad_side(face_flux, dim_index, False)
        )
    return result


def relax(iterate, right_side, conductivity, face_weights, diagonal):
    for sweep_index in range(SWEEPS):
        iterate = (
            iterate
            + RELAXATION * (right_side - operate(iterate, conductivity, face_weights)) / diagonal
        )
    return iterate


def source_field(source_cells, cell_count):
    source_count = source_cells.shape[0]
    row_index = jnp.arange(source_count, dtype=jnp.int32)[:, None] * jnp.ones((1, 2), jnp.int32)
    polarity = jnp.broadcast_to(jnp.array([CURRENT, -CURRENT], jnp.float32), (source_count, 2))
    return (
        jnp.zeros((source_count, cell_count), jnp.float32).at[row_index, source_cells].add(polarity)
    )


def sweep_epoch(model_log, forward, adjoint, sources, receiver_cells, observed):
    grid_shape = forward.shape
    conductivity = jnp.exp(model_log)[None]
    face_weights, diagonal = conductances(conductivity)
    forward = relax(forward, sources.reshape(grid_shape), conductivity, face_weights, diagonal)
    flat_field = forward.reshape(grid_shape[0], -1)
    misfit = flat_field[:, receiver_cells] - observed
    adjoint_source = (
        jnp.zeros_like(flat_field)
        .at[:, receiver_cells]
        .add(DATA_WEIGHT * misfit)
        .reshape(grid_shape)
    )
    adjoint = relax(adjoint, adjoint_source, conductivity, face_weights, diagonal)
    gradient = conductivity[0] * jnp.sum(forward * adjoint, axis=0)
    return (forward, adjoint, gradient)


def temporal_factor(epochs):
    second = (
        jnp.eye(epochs - 2, epochs, dtype=jnp.float32)
        - 2.0 * jnp.eye(epochs - 2, epochs, k=1, dtype=jnp.float32)
        + jnp.eye(epochs - 2, epochs, k=2, dtype=jnp.float32)
    )
    matrix = jnp.eye(epochs, dtype=jnp.float32) + PENALTY * jnp.dot(
        second.T, second, precision=lax.Precision.HIGHEST
    )
    return jnp.linalg.cholesky(matrix)


def difference(values):
    return values[:-2] - 2.0 * values[1:-1] + values[2:]


def difference_adjoint(values):
    widths_low = [(0, 2), (0, 0)]
    widths_mid = [(1, 1), (0, 0)]
    widths_high = [(2, 0), (0, 0)]
    return (
        jnp.pad(values, widths_low)
        - 2.0 * jnp.pad(values, widths_mid)
        + jnp.pad(values, widths_high)
    )


def splitting_update(local_rhs, split_term, dual_term, factor):
    right_side = local_rhs + PENALTY * difference_adjoint(split_term - dual_term)
    updated = jax.scipy.linalg.cho_solve((factor, True), right_side)
    shifted = difference(updated) + dual_term
    split_term = shifted - jnp.clip(shifted, -THRESHOLD, THRESHOLD)
    dual_term = shifted - split_term
    return (updated, split_term, dual_term)


def stencil_kernel(
    size_y,
    model_ref, forward_ref, adjoint_ref, keep_ref, source_ref, receiver_ref, observed_ref,
    out_ref, field_ref, drive_ref,
):
    rows, lanes = model_ref.shape
    conductivity = jnp.exp(model_ref[...])
    row_id = lax.broadcasted_iota(jnp.int32, (rows, lanes), 0)
    lane_id = lax.broadcasted_iota(jnp.int32, (rows, lanes), 1)
    def next_z(v):
        return pltpu.roll(v, lanes - 1, 1)

    def prev_z(v):
        return pltpu.roll(v, 1, 1)

    def next_y(v):
        return pltpu.roll(v, rows - 1, 0)

    def prev_y(v):
        return pltpu.roll(v, 1, 0)

    def next_x(v):
        return jnp.concatenate([v[size_y:], v[:size_y]], axis=0)

    def prev_x(v):
        return jnp.concatenate([v[rows - size_y:], v[: rows - size_y]], axis=0)

    zero = jnp.zeros_like(conductivity)
    weight_x = jnp.where(row_id < rows - size_y, 0.5 * (conductivity + next_x(conductivity)), zero)
    weight_y = jnp.where(row_id % size_y < size_y - 1, 0.5 * (conductivity + next_y(conductivity)), zero)
    weight_z = jnp.where(lane_id < lanes - 1, 0.5 * (conductivity + next_z(conductivity)), zero)
    mass = MASS_TERM * conductivity
    diagonal = mass + weight_x + prev_x(weight_x)
    diagonal = diagonal + weight_y + prev_y(weight_y)
    diagonal = diagonal + weight_z + prev_z(weight_z)

    def operate(v):
        result = mass * v
        flux = weight_x * (next_x(v) - v)
        result = result - flux + prev_x(flux)
        flux = weight_y * (next_y(v) - v)
        result = result - flux + prev_y(flux)
        flux = weight_z * (next_z(v) - v)
        result = result - flux + prev_z(flux)
        return result

    def relax(v, right_side):
        for sweep_index in range(SWEEPS):
            v = v + RELAXATION * (right_side - operate(v)) / diagonal
        return v

    one_row = lax.broadcasted_iota(jnp.int32, (1, lanes), 1)

    def add_at(cell, amount):
        row = cell // lanes
        drive_ref[pl.ds(row, 1), :] += jnp.where(one_row == cell % lanes, amount, 0.0)

    drive_ref[...] = zero
    add_at(source_ref[0], CURRENT)
    add_at(source_ref[1], -CURRENT)
    forward = relax(forward_ref[...], drive_ref[...])
    field_ref[...] = forward
    drive_ref[...] = zero

    def gather_scatter(index, carry):
        cell = receiver_ref[index]
        row = cell // lanes
        hit = one_row == cell % lanes
        value = jnp.sum(jnp.where(hit, field_ref[pl.ds(row, 1), :], 0.0), axis=1, keepdims=True)
        misfit = value - observed_ref[index]
        drive_ref[pl.ds(row, 1), :] += jnp.where(hit, DATA_WEIGHT * misfit, 0.0)
        return carry

    lax.fori_loop(0, receiver_ref.shape[0], gather_scatter, 0)
    adjoint = relax(adjoint_ref[...], drive_ref[...])
    out_ref[...] = keep_ref[0] * model_ref[...] - STEP_SIZE * (conductivity * (forward * adjoint))


def stencil_terms(size_y, model, forward, adjoint, keep, source_cells, receiver_cells, observed):
    rows, lanes = model.shape
    vmem = pl.BlockSpec(memory_space=pltpu.VMEM)
    smem = pl.BlockSpec(memory_space=pltpu.SMEM)
    return pl.pallas_call(
        functools.partial(stencil_kernel, size_y),
        out_shape=jax.ShapeDtypeStruct((rows, lanes), jnp.float32),
        in_specs=[vmem, vmem, vmem, smem, smem, smem, smem],
        out_specs=vmem,
        scratch_shapes=[pltpu.VMEM((rows, lanes), jnp.float32), pltpu.VMEM((rows, lanes), jnp.float32)],
    )(model, forward, adjoint, keep, source_cells, receiver_cells, observed)


def on_device(
    log_conductivity,
    forward_field,
    adjoint_field,
    source_cells,
    receiver_cells,
    observed,
    split_term,
    dual_term,
):
    slab_epochs, size_x, size_y, size_z = log_conductivity.shape
    cell_count = size_x * size_y * size_z
    src_count = lax.axis_size("src")
    ep_count = lax.axis_size("ep")
    devices = src_count * ep_count
    share_cells = cell_count // devices
    share_rows = share_cells // size_z
    total_epochs = slab_epochs * ep_count
    factor = temporal_factor(total_epochs)
    keep = jnp.where(lax.axis_index("src") == 0, 1.0, 0.0).astype(jnp.float32).reshape(1)
    partial_rhs = stencil_terms(
        size_y,
        log_conductivity.reshape(size_x * size_y, size_z),
        forward_field.reshape(size_x * size_y, size_z),
        adjoint_field.reshape(size_x * size_y, size_z),
        keep,
        source_cells.reshape(2),
        receiver_cells,
        observed.reshape(-1),
    )
    sent = partial_rhs.reshape(devices, share_rows, size_z)
    got = lax.all_to_all(sent, ("src", "ep"), split_axis=0, concat_axis=0, tiled=True)
    time_rhs = got.reshape(src_count, total_epochs, share_rows, size_z).sum(axis=0)
    updated, split_term, dual_term = splitting_update(
        time_rhs.reshape(total_epochs, share_cells), split_term, dual_term, factor
    )
    back = jnp.broadcast_to(
        updated.reshape(1, total_epochs, share_rows, size_z),
        (src_count, total_epochs, share_rows, size_z),
    ).reshape(devices, share_rows, size_z)
    model_rows = lax.all_to_all(back, ("src", "ep"), split_axis=0, concat_axis=0, tiled=True)
    model_log = model_rows.reshape(slab_epochs, size_x, size_y, size_z)
    return (model_log, split_term, dual_term)


def solution(mesh):
    return jax.shard_map(
        on_device,
        mesh=mesh,
        in_specs=(
            P("ep", None, None, None),
            P("ep", "src", None, None, None),
            P("ep", "src", None, None, None),
            P("src", None),
            P(),
            P("ep", "src", None),
            P(None, ("src", "ep")),
            P(None, ("src", "ep")),
        ),
        out_specs=(P("ep", None, None, None), P(None, ("src", "ep")), P(None, ("src", "ep"))),
        check_vma=False,
    )
```

```python
import functools

import jax
import jax.numpy as jnp
from jax import lax
from jax.sharding import PartitionSpec as P
from jax.experimental import pallas as pl
from jax.experimental.pallas import tpu as pltpu

SWEEPS = 4


MASS_TERM = 0.5
RELAXATION = 0.8
CURRENT = 4.0
DATA_WEIGHT = 8.0
STEP_SIZE = 0.5
PENALTY = 64.0
THRESHOLD = 0.1


def pad_side(values, dim_index, at_low):
    widths = [(0, 0)] * values.ndim
    widths[dim_index] = (0, 1) if at_low else (1, 0)
    return jnp.pad(values, widths)


def conductances(conductivity):
    face_weights = []
    diagonal = MASS_TERM * conductivity
    ndims = conductivity.ndim
    for dim_index in range(ndims - 3, ndims):
        length = conductivity.shape[dim_index]
        lower_cells = lax.slice_in_dim(conductivity, 0, length - 1, axis=dim_index)
        upper_cells = lax.slice_in_dim(conductivity, 1, length, axis=dim_index)
        face_weight = 0.5 * (lower_cells + upper_cells)
        face_weights.append(face_weight)
        diagonal = (
            diagonal
            + pad_side(face_weight, dim_index, True)
            + pad_side(face_weight, dim_index, False)
        )
    return (face_weights, diagonal)


def operate(iterate, conductivity, face_weights):
    result = MASS_TERM * conductivity * iterate
    ndims = iterate.ndim
    for position, dim_index in enumerate(range(ndims - 3, ndims)):
        length = iterate.shape[dim_index]
        face_flux = face_weights[position] * (
            lax.slice_in_dim(iterate, 1, length, axis=dim_index)
            - lax.slice_in_dim(iterate, 0, length - 1, axis=dim_index)
        )
        result = (
            result - pad_side(face_flux, dim_index, True) + pad_side(face_flux, dim_index, False)
        )
    return result


def relax(iterate, right_side, conductivity, face_weights, diagonal):
    for sweep_index in range(SWEEPS):
        iterate = (
            iterate
            + RELAXATION * (right_side - operate(iterate, conductivity, face_weights)) / diagonal
        )
    return iterate


def source_field(source_cells, cell_count):
    source_count = source_cells.shape[0]
    row_index = jnp.arange(source_count, dtype=jnp.int32)[:, None] * jnp.ones((1, 2), jnp.int32)
    polarity = jnp.broadcast_to(jnp.array([CURRENT, -CURRENT], jnp.float32), (source_count, 2))
    return (
        jnp.zeros((source_count, cell_count), jnp.float32).at[row_index, source_cells].add(polarity)
    )


def sweep_epoch(model_log, forward, adjoint, sources, receiver_cells, observed):
    grid_shape = forward.shape
    conductivity = jnp.exp(model_log)[None]
    face_weights, diagonal = conductances(conductivity)
    forward = relax(forward, sources.reshape(grid_shape), conductivity, face_weights, diagonal)
    flat_field = forward.reshape(grid_shape[0], -1)
    misfit = flat_field[:, receiver_cells] - observed
    adjoint_source = (
        jnp.zeros_like(flat_field)
        .at[:, receiver_cells]
        .add(DATA_WEIGHT * misfit)
        .reshape(grid_shape)
    )
    adjoint = relax(adjoint, adjoint_source, conductivity, face_weights, diagonal)
    gradient = conductivity[0] * jnp.sum(forward * adjoint, axis=0)
    return (forward, adjoint, gradient)


def temporal_factor(epochs):
    second = (
        jnp.eye(epochs - 2, epochs, dtype=jnp.float32)
        - 2.0 * jnp.eye(epochs - 2, epochs, k=1, dtype=jnp.float32)
        + jnp.eye(epochs - 2, epochs, k=2, dtype=jnp.float32)
    )
    matrix = jnp.eye(epochs, dtype=jnp.float32) + PENALTY * jnp.dot(
        second.T, second, precision=lax.Precision.HIGHEST
    )
    return jnp.linalg.cholesky(matrix)


def difference(values):
    return values[:-2] - 2.0 * values[1:-1] + values[2:]


def difference_adjoint(values):
    widths_low = [(0, 2), (0, 0)]
    widths_mid = [(1, 1), (0, 0)]
    widths_high = [(2, 0), (0, 0)]
    return (
        jnp.pad(values, widths_low)
        - 2.0 * jnp.pad(values, widths_mid)
        + jnp.pad(values, widths_high)
    )


def splitting_update(local_rhs, split_term, dual_term, factor):
    right_side = local_rhs + PENALTY * difference_adjoint(split_term - dual_term)
    updated = jax.scipy.linalg.cho_solve((factor, True), right_side)
    shifted = difference(updated) + dual_term
    split_term = shifted - jnp.clip(shifted, -THRESHOLD, THRESHOLD)
    dual_term = shifted - split_term
    return (updated, split_term, dual_term)


def stencil_kernel(
    size_y,
    model_ref, forward_ref, adjoint_ref, receiver_vec_ref, observed_vec_ref,
    keep_ref, source_ref, receiver_ref,
    out_ref, field_ref, drive_ref, picked_ref,
):
    rows, lanes = model_ref.shape
    conductivity = jnp.exp(model_ref[...])
    row_id = lax.broadcasted_iota(jnp.int32, (rows, lanes), 0)
    lane_id = lax.broadcasted_iota(jnp.int32, (rows, lanes), 1)
    def next_z(v):
        return pltpu.roll(v, lanes - 1, 1)

    def prev_z(v):
        return pltpu.roll(v, 1, 1)

    def next_y(v):
        return pltpu.roll(v, rows - 1, 0)

    def prev_y(v):
        return pltpu.roll(v, 1, 0)

    def next_x(v):
        return jnp.concatenate([v[size_y:], v[:size_y]], axis=0)

    def prev_x(v):
        return jnp.concatenate([v[rows - size_y:], v[: rows - size_y]], axis=0)

    zero = jnp.zeros_like(conductivity)
    weight_x = jnp.where(row_id < rows - size_y, 0.5 * (conductivity + next_x(conductivity)), zero)
    weight_y = jnp.where(row_id % size_y < size_y - 1, 0.5 * (conductivity + next_y(conductivity)), zero)
    weight_z = jnp.where(lane_id < lanes - 1, 0.5 * (conductivity + next_z(conductivity)), zero)
    mass = MASS_TERM * conductivity
    diagonal = mass + weight_x + prev_x(weight_x)
    diagonal = diagonal + weight_y + prev_y(weight_y)
    diagonal = diagonal + weight_z + prev_z(weight_z)

    def operate(v):
        result = mass * v
        flux = weight_x * (next_x(v) - v)
        result = result - flux + prev_x(flux)
        flux = weight_y * (next_y(v) - v)
        result = result - flux + prev_y(flux)
        flux = weight_z * (next_z(v) - v)
        result = result - flux + prev_z(flux)
        return result

    def relax(v, right_side):
        for sweep_index in range(SWEEPS):
            v = v + RELAXATION * (right_side - operate(v)) / diagonal
        return v

    one_row = lax.broadcasted_iota(jnp.int32, (1, lanes), 1)

    def add_at(cell, amount):
        row = cell // lanes
        drive_ref[pl.ds(row, 1), :] += jnp.where(one_row == cell % lanes, amount, 0.0)

    drive_ref[...] = zero
    add_at(source_ref[0], CURRENT)
    add_at(source_ref[1], -CURRENT)
    forward = relax(forward_ref[...], drive_ref[...])
    field_ref[...] = forward
    receivers = receiver_ref.shape[0]

    def pick_row(index, carry):
        cell = receiver_ref[index]
        picked_ref[pl.ds(index, 1), :] = field_ref[pl.ds(cell // lanes, 1), :]
        return carry

    lax.fori_loop(0, receivers, pick_row, 0, unroll=8)
    cells = receiver_vec_ref[...]
    picked = picked_ref[...].T
    hit = lax.broadcasted_iota(jnp.int32, (lanes, receivers), 0) == cells % lanes
    value = jnp.sum(jnp.where(hit, picked, 0.0), axis=0, keepdims=True)
    misfit = value - observed_vec_ref[...]
    weighted = jnp.where(hit, DATA_WEIGHT * misfit, 0.0)
    placed = (lax.broadcasted_iota(jnp.int32, (rows, receivers), 0) == cells // lanes).astype(jnp.float32)
    drive = lax.dot_general(
        placed, weighted, (((1,), (1,)), ((), ())),
        precision=lax.Precision.HIGHEST, preferred_element_type=jnp.float32,
    )
    adjoint = relax(adjoint_ref[...], drive)
    out_ref[...] = keep_ref[0] * model_ref[...] - STEP_SIZE * (conductivity * (forward * adjoint))


def stencil_terms(size_y, model, forward, adjoint, keep, source_cells, receiver_cells, observed):
    rows, lanes = model.shape
    receivers = receiver_cells.shape[0]
    vmem = pl.BlockSpec(memory_space=pltpu.VMEM)
    smem = pl.BlockSpec(memory_space=pltpu.SMEM)
    return pl.pallas_call(
        functools.partial(stencil_kernel, size_y),
        out_shape=jax.ShapeDtypeStruct((rows, lanes), jnp.float32),
        in_specs=[vmem, vmem, vmem, vmem, vmem, smem, smem, smem],
        out_specs=vmem,
        scratch_shapes=[
            pltpu.VMEM((rows, lanes), jnp.float32),
            pltpu.VMEM((rows, lanes), jnp.float32),
            pltpu.VMEM((receivers, lanes), jnp.float32),
        ],
    )(
        model, forward, adjoint, receiver_cells.reshape(1, receivers),
        observed.reshape(1, receivers), keep, source_cells, receiver_cells,
    )


def on_device(
    log_conductivity,
    forward_field,
    adjoint_field,
    source_cells,
    receiver_cells,
    observed,
    split_term,
    dual_term,
):
    slab_epochs, size_x, size_y, size_z = log_conductivity.shape
    cell_count = size_x * size_y * size_z
    src_count = lax.axis_size("src")
    ep_count = lax.axis_size("ep")
    devices = src_count * ep_count
    share_cells = cell_count // devices
    share_rows = share_cells // size_z
    total_epochs = slab_epochs * ep_count
    factor = temporal_factor(total_epochs)
    keep = jnp.where(lax.axis_index("src") == 0, 1.0, 0.0).astype(jnp.float32).reshape(1)
    partial_rhs = stencil_terms(
        size_y,
        log_conductivity.reshape(size_x * size_y, size_z),
        forward_field.reshape(size_x * size_y, size_z),
        adjoint_field.reshape(size_x * size_y, size_z),
        keep,
        source_cells.reshape(2),
        receiver_cells,
        observed.reshape(-1),
    )
    sent = partial_rhs.reshape(devices, share_rows, size_z)
    got = lax.all_to_all(sent, ("src", "ep"), split_axis=0, concat_axis=0, tiled=True)
    time_rhs = got.reshape(src_count, total_epochs, share_rows, size_z).sum(axis=0)
    updated, split_term, dual_term = splitting_update(
        time_rhs.reshape(total_epochs, share_cells), split_term, dual_term, factor
    )
    back = jnp.broadcast_to(
        updated.reshape(1, total_epochs, share_rows, size_z),
        (src_count, total_epochs, share_rows, size_z),
    ).reshape(devices, share_rows, size_z)
    model_rows = lax.all_to_all(back, ("src", "ep"), split_axis=0, concat_axis=0, tiled=True)
    model_log = model_rows.reshape(slab_epochs, size_x, size_y, size_z)
    return (model_log, split_term, dual_term)


def solution(mesh):
    return jax.shard_map(
        on_device,
        mesh=mesh,
        in_specs=(
            P("ep", None, None, None),
            P("ep", "src", None, None, None),
            P("ep", "src", None, None, None),
            P("src", None),
            P(),
            P("ep", "src", None),
            P(None, ("src", "ep")),
            P(None, ("src", "ep")),
        ),
        out_specs=(P("ep", None, None, None), P(None, ("src", "ep")), P(None, ("src", "ep"))),
        check_vma=False,
    )
```

```python
import functools

import jax
import jax.numpy as jnp
from jax import lax
from jax.sharding import PartitionSpec as P
from jax.experimental import pallas as pl
from jax.experimental.pallas import tpu as pltpu

SWEEPS = 4


MASS_TERM = 0.5
RELAXATION = 0.8
CURRENT = 4.0
DATA_WEIGHT = 8.0
STEP_SIZE = 0.5
PENALTY = 64.0
THRESHOLD = 0.1


def pad_side(values, dim_index, at_low):
    widths = [(0, 0)] * values.ndim
    widths[dim_index] = (0, 1) if at_low else (1, 0)
    return jnp.pad(values, widths)


def conductances(conductivity):
    face_weights = []
    diagonal = MASS_TERM * conductivity
    ndims = conductivity.ndim
    for dim_index in range(ndims - 3, ndims):
        length = conductivity.shape[dim_index]
        lower_cells = lax.slice_in_dim(conductivity, 0, length - 1, axis=dim_index)
        upper_cells = lax.slice_in_dim(conductivity, 1, length, axis=dim_index)
        face_weight = 0.5 * (lower_cells + upper_cells)
        face_weights.append(face_weight)
        diagonal = (
            diagonal
            + pad_side(face_weight, dim_index, True)
            + pad_side(face_weight, dim_index, False)
        )
    return (face_weights, diagonal)


def operate(iterate, conductivity, face_weights):
    result = MASS_TERM * conductivity * iterate
    ndims = iterate.ndim
    for position, dim_index in enumerate(range(ndims - 3, ndims)):
        length = iterate.shape[dim_index]
        face_flux = face_weights[position] * (
            lax.slice_in_dim(iterate, 1, length, axis=dim_index)
            - lax.slice_in_dim(iterate, 0, length - 1, axis=dim_index)
        )
        result = (
            result - pad_side(face_flux, dim_index, True) + pad_side(face_flux, dim_index, False)
        )
    return result


def relax(iterate, right_side, conductivity, face_weights, diagonal):
    for sweep_index in range(SWEEPS):
        iterate = (
            iterate
            + RELAXATION * (right_side - operate(iterate, conductivity, face_weights)) / diagonal
        )
    return iterate


def source_field(source_cells, cell_count):
    source_count = source_cells.shape[0]
    row_index = jnp.arange(source_count, dtype=jnp.int32)[:, None] * jnp.ones((1, 2), jnp.int32)
    polarity = jnp.broadcast_to(jnp.array([CURRENT, -CURRENT], jnp.float32), (source_count, 2))
    return (
        jnp.zeros((source_count, cell_count), jnp.float32).at[row_index, source_cells].add(polarity)
    )


def sweep_epoch(model_log, forward, adjoint, sources, receiver_cells, observed):
    grid_shape = forward.shape
    conductivity = jnp.exp(model_log)[None]
    face_weights, diagonal = conductances(conductivity)
    forward = relax(forward, sources.reshape(grid_shape), conductivity, face_weights, diagonal)
    flat_field = forward.reshape(grid_shape[0], -1)
    misfit = flat_field[:, receiver_cells] - observed
    adjoint_source = (
        jnp.zeros_like(flat_field)
        .at[:, receiver_cells]
        .add(DATA_WEIGHT * misfit)
        .reshape(grid_shape)
    )
    adjoint = relax(adjoint, adjoint_source, conductivity, face_weights, diagonal)
    gradient = conductivity[0] * jnp.sum(forward * adjoint, axis=0)
    return (forward, adjoint, gradient)


def temporal_factor(epochs):
    second = (
        jnp.eye(epochs - 2, epochs, dtype=jnp.float32)
        - 2.0 * jnp.eye(epochs - 2, epochs, k=1, dtype=jnp.float32)
        + jnp.eye(epochs - 2, epochs, k=2, dtype=jnp.float32)
    )
    matrix = jnp.eye(epochs, dtype=jnp.float32) + PENALTY * jnp.dot(
        second.T, second, precision=lax.Precision.HIGHEST
    )
    return jnp.linalg.cholesky(matrix)


def difference(values):
    return values[:-2] - 2.0 * values[1:-1] + values[2:]


def difference_adjoint(values):
    widths_low = [(0, 2), (0, 0)]
    widths_mid = [(1, 1), (0, 0)]
    widths_high = [(2, 0), (0, 0)]
    return (
        jnp.pad(values, widths_low)
        - 2.0 * jnp.pad(values, widths_mid)
        + jnp.pad(values, widths_high)
    )


def splitting_update(local_rhs, split_term, dual_term, factor):
    right_side = local_rhs + PENALTY * difference_adjoint(split_term - dual_term)
    updated = jax.scipy.linalg.cho_solve((factor, True), right_side)
    shifted = difference(updated) + dual_term
    split_term = shifted - jnp.clip(shifted, -THRESHOLD, THRESHOLD)
    dual_term = shifted - split_term
    return (updated, split_term, dual_term)


def stencil_kernel(
    size_y,
    model_ref, forward_ref, adjoint_ref, receiver_vec_ref, observed_vec_ref,
    keep_ref, source_ref, receiver_ref,
    out_ref, field_ref, drive_ref, picked_ref,
):
    rows, lanes = model_ref.shape
    conductivity = jnp.exp(model_ref[...])
    row_id = lax.broadcasted_iota(jnp.int32, (rows, lanes), 0)
    lane_id = lax.broadcasted_iota(jnp.int32, (rows, lanes), 1)
    def next_z(v):
        return pltpu.roll(v, lanes - 1, 1)

    def prev_z(v):
        return pltpu.roll(v, 1, 1)

    def next_y(v):
        return pltpu.roll(v, rows - 1, 0)

    def prev_y(v):
        return pltpu.roll(v, 1, 0)

    def next_x(v):
        return jnp.concatenate([v[size_y:], v[:size_y]], axis=0)

    def prev_x(v):
        return jnp.concatenate([v[rows - size_y:], v[: rows - size_y]], axis=0)

    zero = jnp.zeros_like(conductivity)
    weight_x = jnp.where(row_id < rows - size_y, 0.5 * (conductivity + next_x(conductivity)), zero)
    weight_y = jnp.where(row_id % size_y < size_y - 1, 0.5 * (conductivity + next_y(conductivity)), zero)
    weight_z = jnp.where(lane_id < lanes - 1, 0.5 * (conductivity + next_z(conductivity)), zero)
    mass = MASS_TERM * conductivity
    diagonal = mass + weight_x + prev_x(weight_x)
    diagonal = diagonal + weight_y + prev_y(weight_y)
    diagonal = diagonal + weight_z + prev_z(weight_z)

    def operate(v):
        result = mass * v
        flux = weight_x * (next_x(v) - v)
        result = result - flux + prev_x(flux)
        flux = weight_y * (next_y(v) - v)
        result = result - flux + prev_y(flux)
        flux = weight_z * (next_z(v) - v)
        result = result - flux + prev_z(flux)
        return result

    def relax(v, right_side):
        for sweep_index in range(SWEEPS):
            v = v + RELAXATION * (right_side - operate(v)) / diagonal
        return v

    one_row = lax.broadcasted_iota(jnp.int32, (1, lanes), 1)

    def add_at(cell, amount):
        row = cell // lanes
        drive_ref[pl.ds(row, 1), :] += jnp.where(one_row == cell % lanes, amount, 0.0)

    drive_ref[...] = zero
    add_at(source_ref[0], CURRENT)
    add_at(source_ref[1], -CURRENT)
    forward = relax(forward_ref[...], drive_ref[...])
    field_ref[...] = forward
    receivers = receiver_ref.shape[0]

    def pick_row(index, carry):
        cell = receiver_ref[index]
        picked_ref[pl.ds(index, 1), :] = field_ref[pl.ds(cell // lanes, 1), :]
        return carry

    lax.fori_loop(0, receivers, pick_row, 0, unroll=8)
    cells = receiver_vec_ref[...]
    picked = picked_ref[...].T
    hit = lax.broadcasted_iota(jnp.int32, (lanes, receivers), 0) == cells % lanes
    value = jnp.sum(jnp.where(hit, picked, 0.0), axis=0, keepdims=True)
    misfit = value - observed_vec_ref[...]
    weighted = jnp.where(hit, DATA_WEIGHT * misfit, 0.0)
    placed = (lax.broadcasted_iota(jnp.int32, (rows, receivers), 0) == cells // lanes).astype(jnp.float32)
    drive = lax.dot_general(
        placed, weighted, (((1,), (1,)), ((), ())),
        precision=lax.Precision.HIGHEST, preferred_element_type=jnp.float32,
    )
    adjoint = relax(adjoint_ref[...], drive)
    out_ref[...] = keep_ref[0] * model_ref[...] - STEP_SIZE * (conductivity * (forward * adjoint))


def stencil_terms(size_y, model, forward, adjoint, keep, source_cells, receiver_cells, observed):
    rows, lanes = model.shape
    receivers = receiver_cells.shape[0]
    vmem = pl.BlockSpec(memory_space=pltpu.VMEM)
    smem = pl.BlockSpec(memory_space=pltpu.SMEM)
    return pl.pallas_call(
        functools.partial(stencil_kernel, size_y),
        out_shape=jax.ShapeDtypeStruct((rows, lanes), jnp.float32),
        in_specs=[vmem, vmem, vmem, vmem, vmem, smem, smem, smem],
        out_specs=vmem,
        scratch_shapes=[
            pltpu.VMEM((rows, lanes), jnp.float32),
            pltpu.VMEM((rows, lanes), jnp.float32),
            pltpu.VMEM((receivers, lanes), jnp.float32),
        ],
    )(
        model, forward, adjoint, receiver_cells.reshape(1, receivers),
        observed.reshape(1, receivers), keep, source_cells, receiver_cells,
    )


def solve_kernel(src_count, got_ref, split_ref, dual_ref, factor_ref, back_ref, split_out_ref, dual_out_ref):
    epochs = factor_ref.shape[0]
    rhs = []
    for t in range(epochs):
        total = got_ref[t]
        for s in range(1, src_count):
            total = total + got_ref[s * epochs + t]
        rhs.append(total)
    gap = [split_ref[k] - dual_ref[k] for k in range(epochs - 2)]
    for t in range(epochs):
        adjoint_term = gap[t] if t < epochs - 2 else jnp.zeros_like(rhs[t])
        if 1 <= t <= epochs - 2:
            adjoint_term = adjoint_term - 2.0 * gap[t - 1]
        if t >= 2:
            adjoint_term = adjoint_term + gap[t - 2]
        rhs[t] = rhs[t] + PENALTY * adjoint_term
    lower = []
    for t in range(epochs):
        total = rhs[t]
        for j in range(t):
            total = total - factor_ref[t, j] * lower[j]
        lower.append(total / factor_ref[t, t])
    solved = [None] * epochs
    for t in reversed(range(epochs)):
        total = lower[t]
        for j in range(t + 1, epochs):
            total = total - factor_ref[j, t] * solved[j]
        solved[t] = total / factor_ref[t, t]
    for k in range(epochs - 2):
        shifted = solved[k] - 2.0 * solved[k + 1] + solved[k + 2] + dual_ref[k]
        split = shifted - jnp.clip(shifted, -THRESHOLD, THRESHOLD)
        split_out_ref[k] = split
        dual_out_ref[k] = shifted - split
    for s in range(src_count):
        for t in range(epochs):
            back_ref[s * epochs + t] = solved[t]


def solve_epochs(src_count, got, split_term, dual_term, factor):
    vmem = pl.BlockSpec(memory_space=pltpu.VMEM)
    smem = pl.BlockSpec(memory_space=pltpu.SMEM)
    return pl.pallas_call(
        functools.partial(solve_kernel, src_count),
        out_shape=(
            jax.ShapeDtypeStruct(got.shape, jnp.float32),
            jax.ShapeDtypeStruct(split_term.shape, jnp.float32),
            jax.ShapeDtypeStruct(dual_term.shape, jnp.float32),
        ),
        in_specs=[vmem, vmem, vmem, smem],
        out_specs=(vmem, vmem, vmem),
    )(got, split_term, dual_term, factor)


def on_device(
    log_conductivity,
    forward_field,
    adjoint_field,
    source_cells,
    receiver_cells,
    observed,
    split_term,
    dual_term,
):
    slab_epochs, size_x, size_y, size_z = log_conductivity.shape
    cell_count = size_x * size_y * size_z
    src_count = lax.axis_size("src")
    ep_count = lax.axis_size("ep")
    devices = src_count * ep_count
    share_cells = cell_count // devices
    share_rows = share_cells // size_z
    total_epochs = slab_epochs * ep_count
    factor = temporal_factor(total_epochs)
    keep = jnp.where(lax.axis_index("src") == 0, 1.0, 0.0).astype(jnp.float32).reshape(1)
    partial_rhs = stencil_terms(
        size_y,
        log_conductivity.reshape(size_x * size_y, size_z),
        forward_field.reshape(size_x * size_y, size_z),
        adjoint_field.reshape(size_x * size_y, size_z),
        keep,
        source_cells.reshape(2),
        receiver_cells,
        observed.reshape(-1),
    )
    sent = partial_rhs.reshape(devices, share_rows, size_z)
    got = lax.all_to_all(sent, ("src", "ep"), split_axis=0, concat_axis=0, tiled=True)
    gaps = split_term.shape[0]
    back, split_rows, dual_rows = solve_epochs(
        src_count,
        got,
        split_term.reshape(gaps, share_rows, size_z),
        dual_term.reshape(gaps, share_rows, size_z),
        factor,
    )
    split_term = split_rows.reshape(gaps, share_cells)
    dual_term = dual_rows.reshape(gaps, share_cells)
    model_rows = lax.all_to_all(back, ("src", "ep"), split_axis=0, concat_axis=0, tiled=True)
    model_log = model_rows.reshape(slab_epochs, size_x, size_y, size_z)
    return (model_log, split_term, dual_term)


def solution(mesh):
    return jax.shard_map(
        on_device,
        mesh=mesh,
        in_specs=(
            P("ep", None, None, None),
            P("ep", "src", None, None, None),
            P("ep", "src", None, None, None),
            P("src", None),
            P(),
            P("ep", "src", None),
            P(None, ("src", "ep")),
            P(None, ("src", "ep")),
        ),
        out_specs=(P("ep", None, None, None), P(None, ("src", "ep")), P(None, ("src", "ep"))),
        check_vma=False,
    )
```

```python
import functools

import jax
import jax.numpy as jnp
from jax import lax
from jax.sharding import PartitionSpec as P
from jax.experimental import pallas as pl
from jax.experimental.pallas import tpu as pltpu

SWEEPS = 4


MASS_TERM = 0.5
RELAXATION = 0.8
CURRENT = 4.0
DATA_WEIGHT = 8.0
STEP_SIZE = 0.5
PENALTY = 64.0
THRESHOLD = 0.1


def pad_side(values, dim_index, at_low):
    widths = [(0, 0)] * values.ndim
    widths[dim_index] = (0, 1) if at_low else (1, 0)
    return jnp.pad(values, widths)


def conductances(conductivity):
    face_weights = []
    diagonal = MASS_TERM * conductivity
    ndims = conductivity.ndim
    for dim_index in range(ndims - 3, ndims):
        length = conductivity.shape[dim_index]
        lower_cells = lax.slice_in_dim(conductivity, 0, length - 1, axis=dim_index)
        upper_cells = lax.slice_in_dim(conductivity, 1, length, axis=dim_index)
        face_weight = 0.5 * (lower_cells + upper_cells)
        face_weights.append(face_weight)
        diagonal = (
            diagonal
            + pad_side(face_weight, dim_index, True)
            + pad_side(face_weight, dim_index, False)
        )
    return (face_weights, diagonal)


def operate(iterate, conductivity, face_weights):
    result = MASS_TERM * conductivity * iterate
    ndims = iterate.ndim
    for position, dim_index in enumerate(range(ndims - 3, ndims)):
        length = iterate.shape[dim_index]
        face_flux = face_weights[position] * (
            lax.slice_in_dim(iterate, 1, length, axis=dim_index)
            - lax.slice_in_dim(iterate, 0, length - 1, axis=dim_index)
        )
        result = (
            result - pad_side(face_flux, dim_index, True) + pad_side(face_flux, dim_index, False)
        )
    return result


def relax(iterate, right_side, conductivity, face_weights, diagonal):
    for sweep_index in range(SWEEPS):
        iterate = (
            iterate
            + RELAXATION * (right_side - operate(iterate, conductivity, face_weights)) / diagonal
        )
    return iterate


def source_field(source_cells, cell_count):
    source_count = source_cells.shape[0]
    row_index = jnp.arange(source_count, dtype=jnp.int32)[:, None] * jnp.ones((1, 2), jnp.int32)
    polarity = jnp.broadcast_to(jnp.array([CURRENT, -CURRENT], jnp.float32), (source_count, 2))
    return (
        jnp.zeros((source_count, cell_count), jnp.float32).at[row_index, source_cells].add(polarity)
    )


def sweep_epoch(model_log, forward, adjoint, sources, receiver_cells, observed):
    grid_shape = forward.shape
    conductivity = jnp.exp(model_log)[None]
    face_weights, diagonal = conductances(conductivity)
    forward = relax(forward, sources.reshape(grid_shape), conductivity, face_weights, diagonal)
    flat_field = forward.reshape(grid_shape[0], -1)
    misfit = flat_field[:, receiver_cells] - observed
    adjoint_source = (
        jnp.zeros_like(flat_field)
        .at[:, receiver_cells]
        .add(DATA_WEIGHT * misfit)
        .reshape(grid_shape)
    )
    adjoint = relax(adjoint, adjoint_source, conductivity, face_weights, diagonal)
    gradient = conductivity[0] * jnp.sum(forward * adjoint, axis=0)
    return (forward, adjoint, gradient)


def temporal_factor(epochs):
    second = (
        jnp.eye(epochs - 2, epochs, dtype=jnp.float32)
        - 2.0 * jnp.eye(epochs - 2, epochs, k=1, dtype=jnp.float32)
        + jnp.eye(epochs - 2, epochs, k=2, dtype=jnp.float32)
    )
    matrix = jnp.eye(epochs, dtype=jnp.float32) + PENALTY * jnp.dot(
        second.T, second, precision=lax.Precision.HIGHEST
    )
    return jnp.linalg.cholesky(matrix)


def difference(values):
    return values[:-2] - 2.0 * values[1:-1] + values[2:]


def difference_adjoint(values):
    widths_low = [(0, 2), (0, 0)]
    widths_mid = [(1, 1), (0, 0)]
    widths_high = [(2, 0), (0, 0)]
    return (
        jnp.pad(values, widths_low)
        - 2.0 * jnp.pad(values, widths_mid)
        + jnp.pad(values, widths_high)
    )


def splitting_update(local_rhs, split_term, dual_term, factor):
    right_side = local_rhs + PENALTY * difference_adjoint(split_term - dual_term)
    updated = jax.scipy.linalg.cho_solve((factor, True), right_side)
    shifted = difference(updated) + dual_term
    split_term = shifted - jnp.clip(shifted, -THRESHOLD, THRESHOLD)
    dual_term = shifted - split_term
    return (updated, split_term, dual_term)


def stencil_kernel(
    size_y,
    model_ref, forward_ref, adjoint_ref, receiver_vec_ref, observed_vec_ref,
    keep_ref, source_ref, receiver_ref,
    out_ref, drive_ref,
):
    rows, lanes = model_ref.shape
    conductivity = jnp.exp(model_ref[...])
    row_id = lax.broadcasted_iota(jnp.int32, (rows, lanes), 0)
    lane_id = lax.broadcasted_iota(jnp.int32, (rows, lanes), 1)
    def next_z(v):
        return pltpu.roll(v, lanes - 1, 1)

    def prev_z(v):
        return pltpu.roll(v, 1, 1)

    def next_y(v):
        return pltpu.roll(v, rows - 1, 0)

    def prev_y(v):
        return pltpu.roll(v, 1, 0)

    def next_x(v):
        return jnp.concatenate([v[size_y:], v[:size_y]], axis=0)

    def prev_x(v):
        return jnp.concatenate([v[rows - size_y:], v[: rows - size_y]], axis=0)

    zero = jnp.zeros_like(conductivity)
    weight_x = jnp.where(row_id < rows - size_y, 0.5 * (conductivity + next_x(conductivity)), zero)
    weight_y = jnp.where(row_id % size_y < size_y - 1, 0.5 * (conductivity + next_y(conductivity)), zero)
    weight_z = jnp.where(lane_id < lanes - 1, 0.5 * (conductivity + next_z(conductivity)), zero)
    mass = MASS_TERM * conductivity
    diagonal = mass + weight_x + prev_x(weight_x)
    diagonal = diagonal + weight_y + prev_y(weight_y)
    diagonal = diagonal + weight_z + prev_z(weight_z)

    def operate(v):
        result = mass * v
        flux = weight_x * (next_x(v) - v)
        result = result - flux + prev_x(flux)
        flux = weight_y * (next_y(v) - v)
        result = result - flux + prev_y(flux)
        flux = weight_z * (next_z(v) - v)
        result = result - flux + prev_z(flux)
        return result

    def relax(v, right_side):
        for sweep_index in range(SWEEPS):
            v = v + RELAXATION * (right_side - operate(v)) / diagonal
        return v

    one_row = lax.broadcasted_iota(jnp.int32, (1, lanes), 1)

    def add_at(cell, amount):
        row = cell // lanes
        drive_ref[pl.ds(row, 1), :] += jnp.where(one_row == cell % lanes, amount, 0.0)

    drive_ref[...] = zero
    add_at(source_ref[0], CURRENT)
    add_at(source_ref[1], -CURRENT)
    forward = relax(forward_ref[...], drive_ref[...])
    receivers = receiver_ref.shape[0]

    cells = receiver_vec_ref[...]
    placed = (lax.broadcasted_iota(jnp.int32, (rows, receivers), 0) == cells // lanes).astype(jnp.float32)
    picked = lax.dot_general(
        forward, placed, (((0,), (0,)), ((), ())),
        precision=lax.Precision.HIGHEST, preferred_element_type=jnp.float32,
    )
    hit = lax.broadcasted_iota(jnp.int32, (lanes, receivers), 0) == cells % lanes
    value = jnp.sum(jnp.where(hit, picked, 0.0), axis=0, keepdims=True)
    misfit = value - observed_vec_ref[...]
    weighted = jnp.where(hit, DATA_WEIGHT * misfit, 0.0)
    drive = lax.dot_general(
        placed, weighted, (((1,), (1,)), ((), ())),
        precision=lax.Precision.HIGHEST, preferred_element_type=jnp.float32,
    )
    adjoint = relax(adjoint_ref[...], drive)
    out_ref[...] = keep_ref[0] * model_ref[...] - STEP_SIZE * (conductivity * (forward * adjoint))


def stencil_terms(size_y, model, forward, adjoint, keep, source_cells, receiver_cells, observed):
    rows, lanes = model.shape
    receivers = receiver_cells.shape[0]
    vmem = pl.BlockSpec(memory_space=pltpu.VMEM)
    smem = pl.BlockSpec(memory_space=pltpu.SMEM)
    return pl.pallas_call(
        functools.partial(stencil_kernel, size_y),
        out_shape=jax.ShapeDtypeStruct((rows, lanes), jnp.float32),
        in_specs=[vmem, vmem, vmem, vmem, vmem, smem, smem, smem],
        out_specs=vmem,
        scratch_shapes=[pltpu.VMEM((rows, lanes), jnp.float32)],
    )(
        model, forward, adjoint, receiver_cells.reshape(1, receivers),
        observed.reshape(1, receivers), keep, source_cells, receiver_cells,
    )


def on_device(
    log_conductivity,
    forward_field,
    adjoint_field,
    source_cells,
    receiver_cells,
    observed,
    split_term,
    dual_term,
):
    slab_epochs, size_x, size_y, size_z = log_conductivity.shape
    cell_count = size_x * size_y * size_z
    src_count = lax.axis_size("src")
    ep_count = lax.axis_size("ep")
    devices = src_count * ep_count
    share_cells = cell_count // devices
    share_rows = share_cells // size_z
    total_epochs = slab_epochs * ep_count
    factor = temporal_factor(total_epochs)
    keep = jnp.where(lax.axis_index("src") == 0, 1.0, 0.0).astype(jnp.float32).reshape(1)
    partial_rhs = stencil_terms(
        size_y,
        log_conductivity.reshape(size_x * size_y, size_z),
        forward_field.reshape(size_x * size_y, size_z),
        adjoint_field.reshape(size_x * size_y, size_z),
        keep,
        source_cells.reshape(2),
        receiver_cells,
        observed.reshape(-1),
    )
    sent = partial_rhs.reshape(devices, share_rows, size_z)
    got = lax.all_to_all(sent, ("src", "ep"), split_axis=0, concat_axis=0, tiled=True)
    time_rhs = got.reshape(src_count, total_epochs, share_rows, size_z).sum(axis=0)
    updated, split_term, dual_term = splitting_update(
        time_rhs.reshape(total_epochs, share_cells), split_term, dual_term, factor
    )
    back = jnp.broadcast_to(
        updated.reshape(1, total_epochs, share_rows, size_z),
        (src_count, total_epochs, share_rows, size_z),
    ).reshape(devices, share_rows, size_z)
    model_rows = lax.all_to_all(back, ("src", "ep"), split_axis=0, concat_axis=0, tiled=True)
    model_log = model_rows.reshape(slab_epochs, size_x, size_y, size_z)
    return (model_log, split_term, dual_term)


def solution(mesh):
    return jax.shard_map(
        on_device,
        mesh=mesh,
        in_specs=(
            P("ep", None, None, None),
            P("ep", "src", None, None, None),
            P("ep", "src", None, None, None),
            P("src", None),
            P(),
            P("ep", "src", None),
            P(None, ("src", "ep")),
            P(None, ("src", "ep")),
        ),
        out_specs=(P("ep", None, None, None), P(None, ("src", "ep")), P(None, ("src", "ep"))),
        check_vma=False,
    )
```

```python
import functools

import jax
import jax.numpy as jnp
import numpy as np
from jax import lax
from jax.sharding import PartitionSpec as P
from jax.experimental import pallas as pl
from jax.experimental.pallas import tpu as pltpu

SWEEPS = 4


MASS_TERM = 0.5
RELAXATION = 0.8
CURRENT = 4.0
DATA_WEIGHT = 8.0
STEP_SIZE = 0.5
PENALTY = 64.0
THRESHOLD = 0.1


def pad_side(values, dim_index, at_low):
    widths = [(0, 0)] * values.ndim
    widths[dim_index] = (0, 1) if at_low else (1, 0)
    return jnp.pad(values, widths)


def conductances(conductivity):
    face_weights = []
    diagonal = MASS_TERM * conductivity
    ndims = conductivity.ndim
    for dim_index in range(ndims - 3, ndims):
        length = conductivity.shape[dim_index]
        lower_cells = lax.slice_in_dim(conductivity, 0, length - 1, axis=dim_index)
        upper_cells = lax.slice_in_dim(conductivity, 1, length, axis=dim_index)
        face_weight = 0.5 * (lower_cells + upper_cells)
        face_weights.append(face_weight)
        diagonal = (
            diagonal
            + pad_side(face_weight, dim_index, True)
            + pad_side(face_weight, dim_index, False)
        )
    return (face_weights, diagonal)


def operate(iterate, conductivity, face_weights):
    result = MASS_TERM * conductivity * iterate
    ndims = iterate.ndim
    for position, dim_index in enumerate(range(ndims - 3, ndims)):
        length = iterate.shape[dim_index]
        face_flux = face_weights[position] * (
            lax.slice_in_dim(iterate, 1, length, axis=dim_index)
            - lax.slice_in_dim(iterate, 0, length - 1, axis=dim_index)
        )
        result = (
            result - pad_side(face_flux, dim_index, True) + pad_side(face_flux, dim_index, False)
        )
    return result


def relax(iterate, right_side, conductivity, face_weights, diagonal):
    for sweep_index in range(SWEEPS):
        iterate = (
            iterate
            + RELAXATION * (right_side - operate(iterate, conductivity, face_weights)) / diagonal
        )
    return iterate


def source_field(source_cells, cell_count):
    source_count = source_cells.shape[0]
    row_index = jnp.arange(source_count, dtype=jnp.int32)[:, None] * jnp.ones((1, 2), jnp.int32)
    polarity = jnp.broadcast_to(jnp.array([CURRENT, -CURRENT], jnp.float32), (source_count, 2))
    return (
        jnp.zeros((source_count, cell_count), jnp.float32).at[row_index, source_cells].add(polarity)
    )


def sweep_epoch(model_log, forward, adjoint, sources, receiver_cells, observed):
    grid_shape = forward.shape
    conductivity = jnp.exp(model_log)[None]
    face_weights, diagonal = conductances(conductivity)
    forward = relax(forward, sources.reshape(grid_shape), conductivity, face_weights, diagonal)
    flat_field = forward.reshape(grid_shape[0], -1)
    misfit = flat_field[:, receiver_cells] - observed
    adjoint_source = (
        jnp.zeros_like(flat_field)
        .at[:, receiver_cells]
        .add(DATA_WEIGHT * misfit)
        .reshape(grid_shape)
    )
    adjoint = relax(adjoint, adjoint_source, conductivity, face_weights, diagonal)
    gradient = conductivity[0] * jnp.sum(forward * adjoint, axis=0)
    return (forward, adjoint, gradient)


def temporal_factor(epochs):
    second = (
        jnp.eye(epochs - 2, epochs, dtype=jnp.float32)
        - 2.0 * jnp.eye(epochs - 2, epochs, k=1, dtype=jnp.float32)
        + jnp.eye(epochs - 2, epochs, k=2, dtype=jnp.float32)
    )
    matrix = jnp.eye(epochs, dtype=jnp.float32) + PENALTY * jnp.dot(
        second.T, second, precision=lax.Precision.HIGHEST
    )
    return jnp.linalg.cholesky(matrix)


def difference(values):
    return values[:-2] - 2.0 * values[1:-1] + values[2:]


def difference_adjoint(values):
    widths_low = [(0, 2), (0, 0)]
    widths_mid = [(1, 1), (0, 0)]
    widths_high = [(2, 0), (0, 0)]
    return (
        jnp.pad(values, widths_low)
        - 2.0 * jnp.pad(values, widths_mid)
        + jnp.pad(values, widths_high)
    )


def splitting_update(local_rhs, split_term, dual_term, factor):
    right_side = local_rhs + PENALTY * difference_adjoint(split_term - dual_term)
    updated = jax.scipy.linalg.cho_solve((factor, True), right_side)
    shifted = difference(updated) + dual_term
    split_term = shifted - jnp.clip(shifted, -THRESHOLD, THRESHOLD)
    dual_term = shifted - split_term
    return (updated, split_term, dual_term)


def stencil_kernel(
    size_y,
    model_ref, forward_ref, adjoint_ref, receiver_vec_ref, observed_vec_ref,
    keep_ref, source_ref, receiver_ref,
    out_ref, drive_ref,
):
    rows, lanes = model_ref.shape
    size_x = rows // size_y
    inner = 8
    parts = size_y // inner
    slab_rows = rows // parts
    shape = (parts, size_x, inner, lanes)

    def load(ref):
        slabs = [ref[pl.ds(part, slab_rows, stride=parts), :] for part in range(parts)]
        return jnp.stack(slabs).reshape(shape)

    def store(ref, v):
        for part in range(parts):
            ref[pl.ds(part, slab_rows, stride=parts), :] = v[part].reshape(slab_rows, lanes)

    def next_z(v):
        return pltpu.roll(v, lanes - 1, 3)

    def prev_z(v):
        return pltpu.roll(v, 1, 3)

    def next_y(v):
        return jnp.concatenate([v[1:], pltpu.roll(v[:1], inner - 1, 2)], axis=0)

    def prev_y(v):
        return jnp.concatenate([pltpu.roll(v[parts - 1:], 1, 2), v[:-1]], axis=0)

    def next_x(v):
        return jnp.concatenate([v[:, 1:], v[:, :1]], axis=1)

    def prev_x(v):
        return jnp.concatenate([v[:, size_x - 1:], v[:, : size_x - 1]], axis=1)

    model = load(model_ref)
    conductivity = jnp.exp(model)
    part_id = lax.broadcasted_iota(jnp.int32, shape, 0)
    x_id = lax.broadcasted_iota(jnp.int32, shape, 1)
    y_id = lax.broadcasted_iota(jnp.int32, shape, 2) * parts + part_id
    z_id = lax.broadcasted_iota(jnp.int32, shape, 3)
    zero = jnp.zeros_like(conductivity)
    weight_x = jnp.where(x_id < size_x - 1, 0.5 * (conductivity + next_x(conductivity)), zero)
    weight_y = jnp.where(y_id < size_y - 1, 0.5 * (conductivity + next_y(conductivity)), zero)
    weight_z = jnp.where(z_id < lanes - 1, 0.5 * (conductivity + next_z(conductivity)), zero)
    mass = MASS_TERM * conductivity
    diagonal = mass + weight_x + prev_x(weight_x)
    diagonal = diagonal + weight_y + prev_y(weight_y)
    diagonal = diagonal + weight_z + prev_z(weight_z)

    def operate(v):
        result = mass * v
        flux = weight_x * (next_x(v) - v)
        result = result - flux + prev_x(flux)
        flux = weight_y * (next_y(v) - v)
        result = result - flux + prev_y(flux)
        flux = weight_z * (next_z(v) - v)
        result = result - flux + prev_z(flux)
        return result

    def relax(v, right_side):
        for sweep_index in range(SWEEPS):
            v = v + RELAXATION * (right_side - operate(v)) / diagonal
        return v

    one_row = lax.broadcasted_iota(jnp.int32, (1, lanes), 1)

    def add_at(cell, amount):
        row = cell // lanes
        y = row % size_y
        slot = ((y % parts) * size_x + row // size_y) * inner + y // parts
        drive_ref[pl.ds(slot, 1), :] += jnp.where(one_row == cell % lanes, amount, 0.0)

    drive_ref[...] = jnp.zeros((rows, lanes), jnp.float32)
    add_at(source_ref[0], CURRENT)
    add_at(source_ref[1], -CURRENT)
    forward = relax(load(forward_ref), drive_ref[...].reshape(shape))
    receivers = receiver_ref.shape[0]

    cells = receiver_vec_ref[...]
    slot_id = lax.broadcasted_iota(jnp.int32, (rows, receivers), 0)
    slot_row = ((slot_id // inner) % size_x) * size_y + (slot_id % inner) * parts + slot_id // (size_x * inner)
    placed = (slot_row == cells // lanes).astype(jnp.float32)
    picked = lax.dot_general(
        forward.reshape(rows, lanes), placed, (((0,), (0,)), ((), ())),
        precision=lax.Precision.HIGHEST, preferred_element_type=jnp.float32,
    )
    hit = lax.broadcasted_iota(jnp.int32, (lanes, receivers), 0) == cells % lanes
    value = jnp.sum(jnp.where(hit, picked, 0.0), axis=0, keepdims=True)
    misfit = value - observed_vec_ref[...]
    weighted = jnp.where(hit, DATA_WEIGHT * misfit, 0.0)
    drive = lax.dot_general(
        placed, weighted, (((1,), (1,)), ((), ())),
        precision=lax.Precision.HIGHEST, preferred_element_type=jnp.float32,
    )
    adjoint = relax(load(adjoint_ref), drive.reshape(shape))
    store(out_ref, keep_ref[0] * model - STEP_SIZE * (conductivity * (forward * adjoint)))


def stencil_terms(size_y, model, forward, adjoint, keep, source_cells, receiver_cells, observed):
    rows, lanes = model.shape
    receivers = receiver_cells.shape[0]
    vmem = pl.BlockSpec(memory_space=pltpu.VMEM)
    smem = pl.BlockSpec(memory_space=pltpu.SMEM)
    return pl.pallas_call(
        functools.partial(stencil_kernel, size_y),
        out_shape=jax.ShapeDtypeStruct((rows, lanes), jnp.float32),
        in_specs=[vmem, vmem, vmem, vmem, vmem, smem, smem, smem],
        out_specs=vmem,
        scratch_shapes=[pltpu.VMEM((rows, lanes), jnp.float32)],
    )(
        model, forward, adjoint, receiver_cells.reshape(1, receivers),
        observed.reshape(1, receivers), keep, source_cells, receiver_cells,
    )


def temporal_operators(epochs, src_count):
    second = np.eye(epochs - 2, epochs) - 2.0 * np.eye(epochs - 2, epochs, k=1) + np.eye(epochs - 2, epochs, k=2)
    inverse = np.linalg.inv(np.eye(epochs) + PENALTY * second.T @ second)
    solve = np.tile(inverse, (src_count, src_count))
    coupling = np.tile(PENALTY * inverse @ second.T, (src_count, 1))
    return jnp.asarray(solve, jnp.float32), jnp.asarray(coupling, jnp.float32)


def on_device(
    log_conductivity,
    forward_field,
    adjoint_field,
    source_cells,
    receiver_cells,
    observed,
    split_term,
    dual_term,
):
    slab_epochs, size_x, size_y, size_z = log_conductivity.shape
    cell_count = size_x * size_y * size_z
    src_count = lax.axis_size("src")
    ep_count = lax.axis_size("ep")
    devices = src_count * ep_count
    share_cells = cell_count // devices
    share_rows = share_cells // size_z
    total_epochs = slab_epochs * ep_count
    keep = jnp.where(lax.axis_index("src") == 0, 1.0, 0.0).astype(jnp.float32).reshape(1)
    partial_rhs = stencil_terms(
        size_y,
        log_conductivity.reshape(size_x * size_y, size_z),
        forward_field.reshape(size_x * size_y, size_z),
        adjoint_field.reshape(size_x * size_y, size_z),
        keep,
        source_cells.reshape(2),
        receiver_cells,
        observed.reshape(-1),
    )
    sent = partial_rhs.reshape(devices, share_rows, size_z)
    got = lax.all_to_all(sent, ("src", "ep"), split_axis=0, concat_axis=0, tiled=True)
    solve, coupling = temporal_operators(total_epochs, src_count)
    gaps = split_term.shape[0]
    gap = (split_term - dual_term).reshape(gaps, share_rows, size_z)
    fixed_part = jnp.einsum("pk,krz->prz", coupling, gap, precision=lax.Precision.HIGHEST)
    back = jnp.einsum("pq,qrz->prz", solve, got, precision=lax.Precision.HIGHEST) + fixed_part
    updated = back[:total_epochs].reshape(total_epochs, share_cells)
    shifted = difference(updated) + dual_term
    split_term = shifted - jnp.clip(shifted, -THRESHOLD, THRESHOLD)
    dual_term = shifted - split_term
    model_rows = lax.all_to_all(back, ("src", "ep"), split_axis=0, concat_axis=0, tiled=True)
    model_log = model_rows.reshape(slab_epochs, size_x, size_y, size_z)
    return (model_log, split_term, dual_term)


def solution(mesh):
    return jax.shard_map(
        on_device,
        mesh=mesh,
        in_specs=(
            P("ep", None, None, None),
            P("ep", "src", None, None, None),
            P("ep", "src", None, None, None),
            P("src", None),
            P(),
            P("ep", "src", None),
            P(None, ("src", "ep")),
            P(None, ("src", "ep")),
        ),
        out_specs=(P("ep", None, None, None), P(None, ("src", "ep")), P(None, ("src", "ep"))),
        check_vma=False,
    )
```

```python
import functools

import jax
import jax.numpy as jnp
import numpy as np
from jax import lax
from jax.sharding import PartitionSpec as P
from jax.experimental import pallas as pl
from jax.experimental.pallas import tpu as pltpu

SWEEPS = 4


MASS_TERM = 0.5
RELAXATION = 0.8
CURRENT = 4.0
DATA_WEIGHT = 8.0
STEP_SIZE = 0.5
PENALTY = 64.0
THRESHOLD = 0.1


def pad_side(values, dim_index, at_low):
    widths = [(0, 0)] * values.ndim
    widths[dim_index] = (0, 1) if at_low else (1, 0)
    return jnp.pad(values, widths)


def conductances(conductivity):
    face_weights = []
    diagonal = MASS_TERM * conductivity
    ndims = conductivity.ndim
    for dim_index in range(ndims - 3, ndims):
        length = conductivity.shape[dim_index]
        lower_cells = lax.slice_in_dim(conductivity, 0, length - 1, axis=dim_index)
        upper_cells = lax.slice_in_dim(conductivity, 1, length, axis=dim_index)
        face_weight = 0.5 * (lower_cells + upper_cells)
        face_weights.append(face_weight)
        diagonal = (
            diagonal
            + pad_side(face_weight, dim_index, True)
            + pad_side(face_weight, dim_index, False)
        )
    return (face_weights, diagonal)


def operate(iterate, conductivity, face_weights):
    result = MASS_TERM * conductivity * iterate
    ndims = iterate.ndim
    for position, dim_index in enumerate(range(ndims - 3, ndims)):
        length = iterate.shape[dim_index]
        face_flux = face_weights[position] * (
            lax.slice_in_dim(iterate, 1, length, axis=dim_index)
            - lax.slice_in_dim(iterate, 0, length - 1, axis=dim_index)
        )
        result = (
            result - pad_side(face_flux, dim_index, True) + pad_side(face_flux, dim_index, False)
        )
    return result


def relax(iterate, right_side, conductivity, face_weights, diagonal):
    for sweep_index in range(SWEEPS):
        iterate = (
            iterate
            + RELAXATION * (right_side - operate(iterate, conductivity, face_weights)) / diagonal
        )
    return iterate


def source_field(source_cells, cell_count):
    source_count = source_cells.shape[0]
    row_index = jnp.arange(source_count, dtype=jnp.int32)[:, None] * jnp.ones((1, 2), jnp.int32)
    polarity = jnp.broadcast_to(jnp.array([CURRENT, -CURRENT], jnp.float32), (source_count, 2))
    return (
        jnp.zeros((source_count, cell_count), jnp.float32).at[row_index, source_cells].add(polarity)
    )


def sweep_epoch(model_log, forward, adjoint, sources, receiver_cells, observed):
    grid_shape = forward.shape
    conductivity = jnp.exp(model_log)[None]
    face_weights, diagonal = conductances(conductivity)
    forward = relax(forward, sources.reshape(grid_shape), conductivity, face_weights, diagonal)
    flat_field = forward.reshape(grid_shape[0], -1)
    misfit = flat_field[:, receiver_cells] - observed
    adjoint_source = (
        jnp.zeros_like(flat_field)
        .at[:, receiver_cells]
        .add(DATA_WEIGHT * misfit)
        .reshape(grid_shape)
    )
    adjoint = relax(adjoint, adjoint_source, conductivity, face_weights, diagonal)
    gradient = conductivity[0] * jnp.sum(forward * adjoint, axis=0)
    return (forward, adjoint, gradient)


def temporal_factor(epochs):
    second = (
        jnp.eye(epochs - 2, epochs, dtype=jnp.float32)
        - 2.0 * jnp.eye(epochs - 2, epochs, k=1, dtype=jnp.float32)
        + jnp.eye(epochs - 2, epochs, k=2, dtype=jnp.float32)
    )
    matrix = jnp.eye(epochs, dtype=jnp.float32) + PENALTY * jnp.dot(
        second.T, second, precision=lax.Precision.HIGHEST
    )
    return jnp.linalg.cholesky(matrix)


def difference(values):
    return values[:-2] - 2.0 * values[1:-1] + values[2:]


def difference_adjoint(values):
    widths_low = [(0, 2), (0, 0)]
    widths_mid = [(1, 1), (0, 0)]
    widths_high = [(2, 0), (0, 0)]
    return (
        jnp.pad(values, widths_low)
        - 2.0 * jnp.pad(values, widths_mid)
        + jnp.pad(values, widths_high)
    )


def splitting_update(local_rhs, split_term, dual_term, factor):
    right_side = local_rhs + PENALTY * difference_adjoint(split_term - dual_term)
    updated = jax.scipy.linalg.cho_solve((factor, True), right_side)
    shifted = difference(updated) + dual_term
    split_term = shifted - jnp.clip(shifted, -THRESHOLD, THRESHOLD)
    dual_term = shifted - split_term
    return (updated, split_term, dual_term)


def stencil_kernel(
    size_y,
    model_ref, forward_ref, adjoint_ref, receiver_vec_ref, observed_vec_ref,
    keep_ref, source_ref, receiver_ref,
    out_ref, drive_ref,
):
    rows, lanes = model_ref.shape
    size_x = rows // size_y
    inner = 8
    parts = size_y // inner
    slab_rows = rows // parts
    shape = (parts, size_x, inner, lanes)

    def load(ref):
        slabs = [ref[pl.ds(part, slab_rows, stride=parts), :] for part in range(parts)]
        return jnp.stack(slabs).reshape(shape)

    def store(ref, v):
        for part in range(parts):
            ref[pl.ds(part, slab_rows, stride=parts), :] = v[part].reshape(slab_rows, lanes)

    def next_z(v):
        return pltpu.roll(v, lanes - 1, 3)

    def prev_z(v):
        return pltpu.roll(v, 1, 3)

    def next_y(v):
        return jnp.concatenate([v[1:], pltpu.roll(v[:1], inner - 1, 2)], axis=0)

    def prev_y(v):
        return jnp.concatenate([pltpu.roll(v[parts - 1:], 1, 2), v[:-1]], axis=0)

    def next_x(v):
        return jnp.concatenate([v[:, 1:], v[:, :1]], axis=1)

    def prev_x(v):
        return jnp.concatenate([v[:, size_x - 1:], v[:, : size_x - 1]], axis=1)

    model = load(model_ref)
    conductivity = jnp.exp(model)
    part_id = lax.broadcasted_iota(jnp.int32, shape, 0)
    x_id = lax.broadcasted_iota(jnp.int32, shape, 1)
    y_id = lax.broadcasted_iota(jnp.int32, shape, 2) * parts + part_id
    z_id = lax.broadcasted_iota(jnp.int32, shape, 3)
    zero = jnp.zeros_like(conductivity)
    weight_x = jnp.where(x_id < size_x - 1, 0.5 * (conductivity + next_x(conductivity)), zero)
    weight_y = jnp.where(y_id < size_y - 1, 0.5 * (conductivity + next_y(conductivity)), zero)
    weight_z = jnp.where(z_id < lanes - 1, 0.5 * (conductivity + next_z(conductivity)), zero)
    mass = MASS_TERM * conductivity
    diagonal = mass + weight_x + prev_x(weight_x)
    diagonal = diagonal + weight_y + prev_y(weight_y)
    diagonal = diagonal + weight_z + prev_z(weight_z)

    def operate(v):
        result = mass * v
        flux = weight_x * (next_x(v) - v)
        result = result - flux + prev_x(flux)
        flux = weight_y * (next_y(v) - v)
        result = result - flux + prev_y(flux)
        flux = weight_z * (next_z(v) - v)
        result = result - flux + prev_z(flux)
        return result

    def relax(v, right_side):
        for sweep_index in range(SWEEPS):
            v = v + RELAXATION * (right_side - operate(v)) / diagonal
        return v

    one_row = lax.broadcasted_iota(jnp.int32, (1, lanes), 1)

    def add_at(cell, amount):
        row = cell // lanes
        y = row % size_y
        slot = ((y % parts) * size_x + row // size_y) * inner + y // parts
        drive_ref[pl.ds(slot, 1), :] += jnp.where(one_row == cell % lanes, amount, 0.0)

    drive_ref[...] = jnp.zeros((rows, lanes), jnp.float32)
    add_at(source_ref[0], CURRENT)
    add_at(source_ref[1], -CURRENT)
    forward = relax(load(forward_ref), drive_ref[...].reshape(shape))
    receivers = receiver_ref.shape[0]

    cells = receiver_vec_ref[...]
    slot_id = lax.broadcasted_iota(jnp.int32, (rows, receivers), 0)
    slot_row = ((slot_id // inner) % size_x) * size_y + (slot_id % inner) * parts + slot_id // (size_x * inner)
    placed = (slot_row == cells // lanes).astype(jnp.float32)
    picked = lax.dot_general(
        forward.reshape(rows, lanes), placed, (((0,), (0,)), ((), ())),
        precision=lax.Precision.HIGHEST, preferred_element_type=jnp.float32,
    )
    hit = lax.broadcasted_iota(jnp.int32, (lanes, receivers), 0) == cells % lanes
    value = jnp.sum(jnp.where(hit, picked, 0.0), axis=0, keepdims=True)
    misfit = value - observed_vec_ref[...]
    weighted = jnp.where(hit, DATA_WEIGHT * misfit, 0.0)
    drive = lax.dot_general(
        placed, weighted, (((1,), (1,)), ((), ())),
        precision=lax.Precision.HIGHEST, preferred_element_type=jnp.float32,
    )
    adjoint = relax(load(adjoint_ref), drive.reshape(shape))
    store(out_ref, keep_ref[0] * model - STEP_SIZE * (conductivity * (forward * adjoint)))


def stencil_terms(size_y, model, forward, adjoint, keep, source_cells, receiver_cells, observed):
    rows, lanes = model.shape
    receivers = receiver_cells.shape[0]
    vmem = pl.BlockSpec(memory_space=pltpu.VMEM)
    smem = pl.BlockSpec(memory_space=pltpu.SMEM)
    return pl.pallas_call(
        functools.partial(stencil_kernel, size_y),
        out_shape=jax.ShapeDtypeStruct((rows, lanes), jnp.float32),
        in_specs=[vmem, vmem, vmem, vmem, vmem, smem, smem, smem],
        out_specs=vmem,
        scratch_shapes=[pltpu.VMEM((rows, lanes), jnp.float32)],
    )(
        model, forward, adjoint, receiver_cells.reshape(1, receivers),
        observed.reshape(1, receivers), keep, source_cells, receiver_cells,
    )


def temporal_operators(epochs):
    second = np.eye(epochs - 2, epochs) - 2.0 * np.eye(epochs - 2, epochs, k=1) + np.eye(epochs - 2, epochs, k=2)
    inverse = np.linalg.inv(np.eye(epochs) + PENALTY * second.T @ second)
    coupling = PENALTY * inverse @ second.T
    return inverse, jnp.asarray(coupling, jnp.float32)


def on_device(
    log_conductivity,
    forward_field,
    adjoint_field,
    source_cells,
    receiver_cells,
    observed,
    split_term,
    dual_term,
):
    slab_epochs, size_x, size_y, size_z = log_conductivity.shape
    cell_count = size_x * size_y * size_z
    src_count = lax.axis_size("src")
    ep_count = lax.axis_size("ep")
    devices = src_count * ep_count
    share_cells = cell_count // devices
    share_rows = share_cells // size_z
    total_epochs = slab_epochs * ep_count
    keep = jnp.where(lax.axis_index("src") == 0, 1.0, 0.0).astype(jnp.float32).reshape(1)
    partial_rhs = stencil_terms(
        size_y,
        log_conductivity.reshape(size_x * size_y, size_z),
        forward_field.reshape(size_x * size_y, size_z),
        adjoint_field.reshape(size_x * size_y, size_z),
        keep,
        source_cells.reshape(2),
        receiver_cells,
        observed.reshape(-1),
    )
    sent = partial_rhs.reshape(devices, share_rows, size_z)
    got = lax.all_to_all(sent, ("src", "ep"), split_axis=0, concat_axis=0, tiled=True)
    inverse, coupling = temporal_operators(total_epochs)
    gaps = split_term.shape[0]
    gap = (split_term - dual_term).reshape(gaps, share_rows, size_z)
    fixed_part = jnp.einsum("pk,krz->prz", coupling, gap, precision=lax.Precision.HIGHEST)
    summed = got[:total_epochs]
    for s in range(1, src_count):
        summed = summed + got[s * total_epochs : (s + 1) * total_epochs]
    weights = jnp.asarray(np.tile(inverse, (src_count, 1)), jnp.float32)
    back = jnp.tile(fixed_part, (src_count, 1, 1))
    for k in range(total_epochs):
        back = back + weights[:, k, None, None] * summed[k][None]
    updated = back[:total_epochs].reshape(total_epochs, share_cells)
    shifted = difference(updated) + dual_term
    split_term = shifted - jnp.clip(shifted, -THRESHOLD, THRESHOLD)
    dual_term = shifted - split_term
    model_rows = lax.all_to_all(back, ("src", "ep"), split_axis=0, concat_axis=0, tiled=True)
    model_log = model_rows.reshape(slab_epochs, size_x, size_y, size_z)
    return (model_log, split_term, dual_term)


def solution(mesh):
    return jax.shard_map(
        on_device,
        mesh=mesh,
        in_specs=(
            P("ep", None, None, None),
            P("ep", "src", None, None, None),
            P("ep", "src", None, None, None),
            P("src", None),
            P(),
            P("ep", "src", None),
            P(None, ("src", "ep")),
            P(None, ("src", "ep")),
        ),
        out_specs=(P("ep", None, None, None), P(None, ("src", "ep")), P(None, ("src", "ep"))),
        check_vma=False,
    )
```

```python
import functools

import jax
import jax.numpy as jnp
import numpy as np
from jax import lax
from jax.sharding import PartitionSpec as P
from jax.experimental import pallas as pl
from jax.experimental.pallas import tpu as pltpu

SWEEPS = 4


MASS_TERM = 0.5
RELAXATION = 0.8
CURRENT = 4.0
DATA_WEIGHT = 8.0
STEP_SIZE = 0.5
PENALTY = 64.0
THRESHOLD = 0.1


def pad_side(values, dim_index, at_low):
    widths = [(0, 0)] * values.ndim
    widths[dim_index] = (0, 1) if at_low else (1, 0)
    return jnp.pad(values, widths)


def conductances(conductivity):
    face_weights = []
    diagonal = MASS_TERM * conductivity
    ndims = conductivity.ndim
    for dim_index in range(ndims - 3, ndims):
        length = conductivity.shape[dim_index]
        lower_cells = lax.slice_in_dim(conductivity, 0, length - 1, axis=dim_index)
        upper_cells = lax.slice_in_dim(conductivity, 1, length, axis=dim_index)
        face_weight = 0.5 * (lower_cells + upper_cells)
        face_weights.append(face_weight)
        diagonal = (
            diagonal
            + pad_side(face_weight, dim_index, True)
            + pad_side(face_weight, dim_index, False)
        )
    return (face_weights, diagonal)


def operate(iterate, conductivity, face_weights):
    result = MASS_TERM * conductivity * iterate
    ndims = iterate.ndim
    for position, dim_index in enumerate(range(ndims - 3, ndims)):
        length = iterate.shape[dim_index]
        face_flux = face_weights[position] * (
            lax.slice_in_dim(iterate, 1, length, axis=dim_index)
            - lax.slice_in_dim(iterate, 0, length - 1, axis=dim_index)
        )
        result = (
            result - pad_side(face_flux, dim_index, True) + pad_side(face_flux, dim_index, False)
        )
    return result


def relax(iterate, right_side, conductivity, face_weights, diagonal):
    for sweep_index in range(SWEEPS):
        iterate = (
            iterate
            + RELAXATION * (right_side - operate(iterate, conductivity, face_weights)) / diagonal
        )
    return iterate


def source_field(source_cells, cell_count):
    source_count = source_cells.shape[0]
    row_index = jnp.arange(source_count, dtype=jnp.int32)[:, None] * jnp.ones((1, 2), jnp.int32)
    polarity = jnp.broadcast_to(jnp.array([CURRENT, -CURRENT], jnp.float32), (source_count, 2))
    return (
        jnp.zeros((source_count, cell_count), jnp.float32).at[row_index, source_cells].add(polarity)
    )


def sweep_epoch(model_log, forward, adjoint, sources, receiver_cells, observed):
    grid_shape = forward.shape
    conductivity = jnp.exp(model_log)[None]
    face_weights, diagonal = conductances(conductivity)
    forward = relax(forward, sources.reshape(grid_shape), conductivity, face_weights, diagonal)
    flat_field = forward.reshape(grid_shape[0], -1)
    misfit = flat_field[:, receiver_cells] - observed
    adjoint_source = (
        jnp.zeros_like(flat_field)
        .at[:, receiver_cells]
        .add(DATA_WEIGHT * misfit)
        .reshape(grid_shape)
    )
    adjoint = relax(adjoint, adjoint_source, conductivity, face_weights, diagonal)
    gradient = conductivity[0] * jnp.sum(forward * adjoint, axis=0)
    return (forward, adjoint, gradient)


def temporal_factor(epochs):
    second = (
        jnp.eye(epochs - 2, epochs, dtype=jnp.float32)
        - 2.0 * jnp.eye(epochs - 2, epochs, k=1, dtype=jnp.float32)
        + jnp.eye(epochs - 2, epochs, k=2, dtype=jnp.float32)
    )
    matrix = jnp.eye(epochs, dtype=jnp.float32) + PENALTY * jnp.dot(
        second.T, second, precision=lax.Precision.HIGHEST
    )
    return jnp.linalg.cholesky(matrix)


def difference(values):
    return values[:-2] - 2.0 * values[1:-1] + values[2:]


def difference_adjoint(values):
    widths_low = [(0, 2), (0, 0)]
    widths_mid = [(1, 1), (0, 0)]
    widths_high = [(2, 0), (0, 0)]
    return (
        jnp.pad(values, widths_low)
        - 2.0 * jnp.pad(values, widths_mid)
        + jnp.pad(values, widths_high)
    )


def splitting_update(local_rhs, split_term, dual_term, factor):
    right_side = local_rhs + PENALTY * difference_adjoint(split_term - dual_term)
    updated = jax.scipy.linalg.cho_solve((factor, True), right_side)
    shifted = difference(updated) + dual_term
    split_term = shifted - jnp.clip(shifted, -THRESHOLD, THRESHOLD)
    dual_term = shifted - split_term
    return (updated, split_term, dual_term)


def stencil_kernel(
    size_y,
    model_ref, forward_ref, adjoint_ref, receiver_vec_ref, observed_vec_ref,
    keep_ref, source_ref, receiver_ref,
    out_ref, drive_ref,
):
    rows, lanes = model_ref.shape
    size_x = rows // size_y
    inner = 8
    parts = size_y // inner
    slab_rows = rows // parts
    shape = (parts, size_x, inner, lanes)

    def load(ref):
        slabs = [ref[pl.ds(part, slab_rows, stride=parts), :] for part in range(parts)]
        return jnp.stack(slabs).reshape(shape)

    def store(ref, v):
        for part in range(parts):
            ref[pl.ds(part, slab_rows, stride=parts), :] = v[part].reshape(slab_rows, lanes)

    def next_z(v):
        return pltpu.roll(v, lanes - 1, 3)

    def prev_z(v):
        return pltpu.roll(v, 1, 3)

    def next_y(v):
        return jnp.concatenate([v[1:], pltpu.roll(v[:1], inner - 1, 2)], axis=0)

    def prev_y(v):
        return jnp.concatenate([pltpu.roll(v[parts - 1:], 1, 2), v[:-1]], axis=0)

    def next_x(v):
        return jnp.concatenate([v[:, 1:], v[:, :1]], axis=1)

    def prev_x(v):
        return jnp.concatenate([v[:, size_x - 1:], v[:, : size_x - 1]], axis=1)

    model = load(model_ref)
    conductivity = jnp.exp(model)
    part_id = lax.broadcasted_iota(jnp.int32, shape, 0)
    x_id = lax.broadcasted_iota(jnp.int32, shape, 1)
    y_id = lax.broadcasted_iota(jnp.int32, shape, 2) * parts + part_id
    z_id = lax.broadcasted_iota(jnp.int32, shape, 3)
    zero = jnp.zeros_like(conductivity)
    weight_x = jnp.where(x_id < size_x - 1, 0.5 * (conductivity + next_x(conductivity)), zero)
    weight_y = jnp.where(y_id < size_y - 1, 0.5 * (conductivity + next_y(conductivity)), zero)
    weight_z = jnp.where(z_id < lanes - 1, 0.5 * (conductivity + next_z(conductivity)), zero)
    mass = MASS_TERM * conductivity
    diagonal = mass + weight_x + prev_x(weight_x)
    diagonal = diagonal + weight_y + prev_y(weight_y)
    diagonal = diagonal + weight_z + prev_z(weight_z)

    def operate(v):
        result = mass * v
        flux = weight_x * (next_x(v) - v)
        result = result - flux + prev_x(flux)
        flux = weight_y * (next_y(v) - v)
        result = result - flux + prev_y(flux)
        flux = weight_z * (next_z(v) - v)
        result = result - flux + prev_z(flux)
        return result

    def relax(v, right_side):
        for sweep_index in range(SWEEPS):
            v = v + RELAXATION * (right_side - operate(v)) / diagonal
        return v

    one_row = lax.broadcasted_iota(jnp.int32, (1, lanes), 1)

    def add_at(cell, amount):
        row = cell // lanes
        y = row % size_y
        slot = ((y % parts) * size_x + row // size_y) * inner + y // parts
        drive_ref[pl.ds(slot, 1), :] += jnp.where(one_row == cell % lanes, amount, 0.0)

    drive_ref[...] = jnp.zeros((rows, lanes), jnp.float32)
    add_at(source_ref[0], CURRENT)
    add_at(source_ref[1], -CURRENT)
    forward = relax(load(forward_ref), drive_ref[...].reshape(shape))
    receivers = receiver_ref.shape[0]

    cells = receiver_vec_ref[...]
    slot_id = lax.broadcasted_iota(jnp.int32, (rows, receivers), 0)
    slot_row = ((slot_id // inner) % size_x) * size_y + (slot_id % inner) * parts + slot_id // (size_x * inner)
    placed = (slot_row == cells // lanes).astype(jnp.float32)
    picked = lax.dot_general(
        forward.reshape(rows, lanes), placed, (((0,), (0,)), ((), ())),
        precision=lax.Precision.HIGHEST, preferred_element_type=jnp.float32,
    )
    hit = lax.broadcasted_iota(jnp.int32, (lanes, receivers), 0) == cells % lanes
    value = jnp.sum(jnp.where(hit, picked, 0.0), axis=0, keepdims=True)
    misfit = value - observed_vec_ref[...]
    weighted = jnp.where(hit, DATA_WEIGHT * misfit, 0.0)
    drive = lax.dot_general(
        placed, weighted, (((1,), (1,)), ((), ())),
        precision=lax.Precision.HIGHEST, preferred_element_type=jnp.float32,
    )
    adjoint = relax(load(adjoint_ref), drive.reshape(shape))
    store(out_ref, keep_ref[0] * model - STEP_SIZE * (conductivity * (forward * adjoint)))


def stencil_terms(size_y, model, forward, adjoint, keep, source_cells, receiver_cells, observed):
    rows, lanes = model.shape
    receivers = receiver_cells.shape[0]
    vmem = pl.BlockSpec(memory_space=pltpu.VMEM)
    smem = pl.BlockSpec(memory_space=pltpu.SMEM)
    return pl.pallas_call(
        functools.partial(stencil_kernel, size_y),
        out_shape=jax.ShapeDtypeStruct((rows, lanes), jnp.float32),
        in_specs=[vmem, vmem, vmem, vmem, vmem, smem, smem, smem],
        out_specs=vmem,
        scratch_shapes=[pltpu.VMEM((rows, lanes), jnp.float32)],
    )(
        model, forward, adjoint, receiver_cells.reshape(1, receivers),
        observed.reshape(1, receivers), keep, source_cells, receiver_cells,
    )


def temporal_operators(epochs, src_count):
    second = np.eye(epochs - 2, epochs) - 2.0 * np.eye(epochs - 2, epochs, k=1) + np.eye(epochs - 2, epochs, k=2)
    inverse = np.linalg.inv(np.eye(epochs) + PENALTY * second.T @ second)
    solve = np.tile(inverse, (src_count, src_count))
    coupling = np.tile(PENALTY * inverse @ second.T, (src_count, 1))
    return jnp.asarray(solve, jnp.float32), jnp.asarray(coupling, jnp.float32)


def on_device(
    log_conductivity,
    forward_field,
    adjoint_field,
    source_cells,
    receiver_cells,
    observed,
    split_term,
    dual_term,
):
    slab_epochs, size_x, size_y, size_z = log_conductivity.shape
    cell_count = size_x * size_y * size_z
    src_count = lax.axis_size("src")
    ep_count = lax.axis_size("ep")
    devices = src_count * ep_count
    share_cells = cell_count // devices
    share_rows = share_cells // size_z
    total_epochs = slab_epochs * ep_count
    keep = jnp.where(lax.axis_index("src") == 0, 1.0, 0.0).astype(jnp.float32).reshape(1)
    partial_rhs = stencil_terms(
        size_y,
        log_conductivity.reshape(size_x * size_y, size_z),
        forward_field.reshape(size_x * size_y, size_z),
        adjoint_field.reshape(size_x * size_y, size_z),
        keep,
        source_cells.reshape(2),
        receiver_cells,
        observed.reshape(-1),
    )
    sent = partial_rhs.reshape(devices, share_rows, size_z)
    got = lax.all_to_all(sent, ("src", "ep"), split_axis=0, concat_axis=0, tiled=True)
    solve, coupling = temporal_operators(total_epochs, src_count)
    gaps = split_term.shape[0]
    gap = (split_term - dual_term).reshape(gaps, share_rows, size_z)
    fixed_part = jnp.einsum("pk,krz->prz", coupling, gap, precision=lax.Precision.HIGHEST)
    back = jnp.einsum("pq,qrz->prz", solve, got, precision=lax.Precision.HIGHEST) + fixed_part
    updated = back[:total_epochs].reshape(total_epochs, share_cells)
    shifted = difference(updated) + dual_term
    split_term = shifted - jnp.clip(shifted, -THRESHOLD, THRESHOLD)
    dual_term = shifted - split_term
    half = share_rows // 2
    if share_rows % 2 == 0 and src_count % 2 == 0:
        core = lax.axis_index("src") % 2
        own_rows = back[:total_epochs].reshape(total_epochs, 2, half, size_z).transpose(1, 0, 2, 3)
        halves = jnp.broadcast_to(own_rows[None], (src_count // 2,) + own_rows.shape).reshape(devices, half, size_z)
        mine = lax.all_to_all(halves, ("src", "ep"), split_axis=0, concat_axis=0, tiled=True)
        theirs = lax.ppermute(mine, "src", [(i, i ^ 1) for i in range(src_count)])
        model_rows = jnp.where(
            core == 0, jnp.concatenate([mine, theirs], axis=1), jnp.concatenate([theirs, mine], axis=1)
        )
    else:
        model_rows = lax.all_to_all(back, ("src", "ep"), split_axis=0, concat_axis=0, tiled=True)
    model_log = model_rows.reshape(slab_epochs, size_x, size_y, size_z)
    return (model_log, split_term, dual_term)


def solution(mesh):
    return jax.shard_map(
        on_device,
        mesh=mesh,
        in_specs=(
            P("ep", None, None, None),
            P("ep", "src", None, None, None),
            P("ep", "src", None, None, None),
            P("src", None),
            P(),
            P("ep", "src", None),
            P(None, ("src", "ep")),
            P(None, ("src", "ep")),
        ),
        out_specs=(P("ep", None, None, None), P(None, ("src", "ep")), P(None, ("src", "ep"))),
        check_vma=False,
    )
```

```python
import functools

import jax
import jax.numpy as jnp
import numpy as np
from jax import lax
from jax.sharding import PartitionSpec as P
from jax.experimental import pallas as pl
from jax.experimental.pallas import tpu as pltpu

SWEEPS = 4


MASS_TERM = 0.5
RELAXATION = 0.8
CURRENT = 4.0
DATA_WEIGHT = 8.0
STEP_SIZE = 0.5
PENALTY = 64.0
THRESHOLD = 0.1


def pad_side(values, dim_index, at_low):
    widths = [(0, 0)] * values.ndim
    widths[dim_index] = (0, 1) if at_low else (1, 0)
    return jnp.pad(values, widths)


def conductances(conductivity):
    face_weights = []
    diagonal = MASS_TERM * conductivity
    ndims = conductivity.ndim
    for dim_index in range(ndims - 3, ndims):
        length = conductivity.shape[dim_index]
        lower_cells = lax.slice_in_dim(conductivity, 0, length - 1, axis=dim_index)
        upper_cells = lax.slice_in_dim(conductivity, 1, length, axis=dim_index)
        face_weight = 0.5 * (lower_cells + upper_cells)
        face_weights.append(face_weight)
        diagonal = (
            diagonal
            + pad_side(face_weight, dim_index, True)
            + pad_side(face_weight, dim_index, False)
        )
    return (face_weights, diagonal)


def operate(iterate, conductivity, face_weights):
    result = MASS_TERM * conductivity * iterate
    ndims = iterate.ndim
    for position, dim_index in enumerate(range(ndims - 3, ndims)):
        length = iterate.shape[dim_index]
        face_flux = face_weights[position] * (
            lax.slice_in_dim(iterate, 1, length, axis=dim_index)
            - lax.slice_in_dim(iterate, 0, length - 1, axis=dim_index)
        )
        result = (
            result - pad_side(face_flux, dim_index, True) + pad_side(face_flux, dim_index, False)
        )
    return result


def relax(iterate, right_side, conductivity, face_weights, diagonal):
    for sweep_index in range(SWEEPS):
        iterate = (
            iterate
            + RELAXATION * (right_side - operate(iterate, conductivity, face_weights)) / diagonal
        )
    return iterate


def source_field(source_cells, cell_count):
    source_count = source_cells.shape[0]
    row_index = jnp.arange(source_count, dtype=jnp.int32)[:, None] * jnp.ones((1, 2), jnp.int32)
    polarity = jnp.broadcast_to(jnp.array([CURRENT, -CURRENT], jnp.float32), (source_count, 2))
    return (
        jnp.zeros((source_count, cell_count), jnp.float32).at[row_index, source_cells].add(polarity)
    )


def sweep_epoch(model_log, forward, adjoint, sources, receiver_cells, observed):
    grid_shape = forward.shape
    conductivity = jnp.exp(model_log)[None]
    face_weights, diagonal = conductances(conductivity)
    forward = relax(forward, sources.reshape(grid_shape), conductivity, face_weights, diagonal)
    flat_field = forward.reshape(grid_shape[0], -1)
    misfit = flat_field[:, receiver_cells] - observed
    adjoint_source = (
        jnp.zeros_like(flat_field)
        .at[:, receiver_cells]
        .add(DATA_WEIGHT * misfit)
        .reshape(grid_shape)
    )
    adjoint = relax(adjoint, adjoint_source, conductivity, face_weights, diagonal)
    gradient = conductivity[0] * jnp.sum(forward * adjoint, axis=0)
    return (forward, adjoint, gradient)


def temporal_factor(epochs):
    second = (
        jnp.eye(epochs - 2, epochs, dtype=jnp.float32)
        - 2.0 * jnp.eye(epochs - 2, epochs, k=1, dtype=jnp.float32)
        + jnp.eye(epochs - 2, epochs, k=2, dtype=jnp.float32)
    )
    matrix = jnp.eye(epochs, dtype=jnp.float32) + PENALTY * jnp.dot(
        second.T, second, precision=lax.Precision.HIGHEST
    )
    return jnp.linalg.cholesky(matrix)


def difference(values):
    return values[:-2] - 2.0 * values[1:-1] + values[2:]


def difference_adjoint(values):
    widths_low = [(0, 2), (0, 0)]
    widths_mid = [(1, 1), (0, 0)]
    widths_high = [(2, 0), (0, 0)]
    return (
        jnp.pad(values, widths_low)
        - 2.0 * jnp.pad(values, widths_mid)
        + jnp.pad(values, widths_high)
    )


def splitting_update(local_rhs, split_term, dual_term, factor):
    right_side = local_rhs + PENALTY * difference_adjoint(split_term - dual_term)
    updated = jax.scipy.linalg.cho_solve((factor, True), right_side)
    shifted = difference(updated) + dual_term
    split_term = shifted - jnp.clip(shifted, -THRESHOLD, THRESHOLD)
    dual_term = shifted - split_term
    return (updated, split_term, dual_term)


def stencil_kernel(
    size_y,
    half,
    model_ref, forward_ref, adjoint_ref, receiver_vec_ref, observed_vec_ref,
    keep_ref, core_ref, source_ref, receiver_ref,
    *outputs,
):
    drive_ref = outputs[-1]
    rows, lanes = model_ref.shape
    size_x = rows // size_y
    inner = 8
    parts = size_y // inner
    slab_rows = rows // parts
    shape = (parts, size_x, inner, lanes)

    def load(ref):
        slabs = [ref[pl.ds(part, slab_rows, stride=parts), :] for part in range(parts)]
        return jnp.stack(slabs).reshape(shape)

    def store(ref, v):
        for part in range(parts):
            ref[pl.ds(part, slab_rows, stride=parts), :] = v[part].reshape(slab_rows, lanes)

    def next_z(v):
        return pltpu.roll(v, lanes - 1, 3)

    def prev_z(v):
        return pltpu.roll(v, 1, 3)

    def next_y(v):
        return jnp.concatenate([v[1:], pltpu.roll(v[:1], inner - 1, 2)], axis=0)

    def prev_y(v):
        return jnp.concatenate([pltpu.roll(v[parts - 1:], 1, 2), v[:-1]], axis=0)

    def next_x(v):
        return jnp.concatenate([v[:, 1:], v[:, :1]], axis=1)

    def prev_x(v):
        return jnp.concatenate([v[:, size_x - 1:], v[:, : size_x - 1]], axis=1)

    model = load(model_ref)
    conductivity = jnp.exp(model)
    part_id = lax.broadcasted_iota(jnp.int32, shape, 0)
    x_id = lax.broadcasted_iota(jnp.int32, shape, 1)
    y_id = lax.broadcasted_iota(jnp.int32, shape, 2) * parts + part_id
    z_id = lax.broadcasted_iota(jnp.int32, shape, 3)
    zero = jnp.zeros_like(conductivity)
    weight_x = jnp.where(x_id < size_x - 1, 0.5 * (conductivity + next_x(conductivity)), zero)
    weight_y = jnp.where(y_id < size_y - 1, 0.5 * (conductivity + next_y(conductivity)), zero)
    weight_z = jnp.where(z_id < lanes - 1, 0.5 * (conductivity + next_z(conductivity)), zero)
    mass = MASS_TERM * conductivity
    diagonal = mass + weight_x + prev_x(weight_x)
    diagonal = diagonal + weight_y + prev_y(weight_y)
    diagonal = diagonal + weight_z + prev_z(weight_z)

    def operate(v):
        result = mass * v
        flux = weight_x * (next_x(v) - v)
        result = result - flux + prev_x(flux)
        flux = weight_y * (next_y(v) - v)
        result = result - flux + prev_y(flux)
        flux = weight_z * (next_z(v) - v)
        result = result - flux + prev_z(flux)
        return result

    def relax(v, right_side):
        for sweep_index in range(SWEEPS):
            v = v + RELAXATION * (right_side - operate(v)) / diagonal
        return v

    one_row = lax.broadcasted_iota(jnp.int32, (1, lanes), 1)

    def add_at(cell, amount):
        row = cell // lanes
        y = row % size_y
        slot = ((y % parts) * size_x + row // size_y) * inner + y // parts
        drive_ref[pl.ds(slot, 1), :] += jnp.where(one_row == cell % lanes, amount, 0.0)

    drive_ref[...] = jnp.zeros((rows, lanes), jnp.float32)
    add_at(source_ref[0], CURRENT)
    add_at(source_ref[1], -CURRENT)
    forward = relax(load(forward_ref), drive_ref[...].reshape(shape))
    receivers = receiver_ref.shape[0]

    cells = receiver_vec_ref[...]
    slot_id = lax.broadcasted_iota(jnp.int32, (rows, receivers), 0)
    slot_row = ((slot_id // inner) % size_x) * size_y + (slot_id % inner) * parts + slot_id // (size_x * inner)
    placed = (slot_row == cells // lanes).astype(jnp.float32)
    picked = lax.dot_general(
        forward.reshape(rows, lanes), placed, (((0,), (0,)), ((), ())),
        precision=lax.Precision.HIGHEST, preferred_element_type=jnp.float32,
    )
    hit = lax.broadcasted_iota(jnp.int32, (lanes, receivers), 0) == cells % lanes
    value = jnp.sum(jnp.where(hit, picked, 0.0), axis=0, keepdims=True)
    misfit = value - observed_vec_ref[...]
    weighted = jnp.where(hit, DATA_WEIGHT * misfit, 0.0)
    drive = lax.dot_general(
        placed, weighted, (((1,), (1,)), ((), ())),
        precision=lax.Precision.HIGHEST, preferred_element_type=jnp.float32,
    )
    adjoint = relax(load(adjoint_ref), drive.reshape(shape))
    terms = keep_ref[0] * model - STEP_SIZE * (conductivity * (forward * adjoint))
    if not half:
        store(outputs[0], terms)
        return
    keep_out, send_out = outputs[0], outputs[1]
    store(drive_ref, terms)
    core = core_ref[0]
    for chunk in range(keep_out.shape[0]):
        start = chunk * 2 * half
        keep_out[chunk] = drive_ref[pl.ds(pl.multiple_of(start + core * half, half), half), :]
        send_out[chunk] = drive_ref[pl.ds(pl.multiple_of(start + (1 - core) * half, half), half), :]


def stencil_terms(size_y, half, model, forward, adjoint, keep, core, source_cells, receiver_cells, observed):
    rows, lanes = model.shape
    receivers = receiver_cells.shape[0]
    vmem = pl.BlockSpec(memory_space=pltpu.VMEM)
    smem = pl.BlockSpec(memory_space=pltpu.SMEM)
    if half:
        chunks = rows // (2 * half)
        out_shape = (jax.ShapeDtypeStruct((chunks, half, lanes), jnp.float32),) * 2
        out_specs = (vmem, vmem)
    else:
        out_shape = jax.ShapeDtypeStruct((rows, lanes), jnp.float32)
        out_specs = vmem
    return pl.pallas_call(
        functools.partial(stencil_kernel, size_y, half),
        out_shape=out_shape,
        in_specs=[vmem, vmem, vmem, vmem, vmem, smem, smem, smem, smem],
        out_specs=out_specs,
        scratch_shapes=[pltpu.VMEM((rows, lanes), jnp.float32)],
    )(
        model, forward, adjoint, receiver_cells.reshape(1, receivers),
        observed.reshape(1, receivers), keep, core, source_cells, receiver_cells,
    )


def temporal_operators(epochs):
    second = np.eye(epochs - 2, epochs) - 2.0 * np.eye(epochs - 2, epochs, k=1) + np.eye(epochs - 2, epochs, k=2)
    inverse = np.linalg.inv(np.eye(epochs) + PENALTY * second.T @ second)
    coupling = PENALTY * inverse @ second.T
    return inverse.astype(np.float32), coupling.astype(np.float32)


def on_device(
    log_conductivity,
    forward_field,
    adjoint_field,
    source_cells,
    receiver_cells,
    observed,
    split_term,
    dual_term,
):
    slab_epochs, size_x, size_y, size_z = log_conductivity.shape
    cell_count = size_x * size_y * size_z
    src_count = lax.axis_size("src")
    ep_count = lax.axis_size("ep")
    devices = src_count * ep_count
    share_cells = cell_count // devices
    share_rows = share_cells // size_z
    total_epochs = slab_epochs * ep_count
    gaps = split_term.shape[0]
    inverse, coupling = temporal_operators(total_epochs)
    gap = (split_term - dual_term).reshape(gaps, share_rows, size_z)
    fixed_part = jnp.einsum("pk,krz->prz", coupling, gap, precision=lax.Precision.HIGHEST)
    src_index = lax.axis_index("src")
    keep = jnp.where(src_index == 0, 1.0, 0.0).astype(jnp.float32).reshape(1)
    core = (src_index % 2).astype(jnp.int32)
    pairs = [(i, i ^ 1) for i in range(src_count)]
    half = share_rows // 2 if share_rows % 2 == 0 and src_count % 2 == 0 else 0
    terms = stencil_terms(
        size_y,
        half,
        log_conductivity.reshape(size_x * size_y, size_z),
        forward_field.reshape(size_x * size_y, size_z),
        adjoint_field.reshape(size_x * size_y, size_z),
        keep,
        core.reshape(1),
        source_cells.reshape(2),
        receiver_cells,
        observed.reshape(-1),
    )
    if half:
        kept, sent = terms
        summed = kept + lax.ppermute(sent, "src", pairs)
        got = lax.all_to_all(summed, ("src", "ep"), split_axis=0, concat_axis=0, tiled=True)
        rows_by_half = got.reshape(src_count // 2, 2, total_epochs, half, size_z).sum(axis=0)
        fixed_by_half = fixed_part.reshape(total_epochs, 2, half, size_z).transpose(1, 0, 2, 3)
        solved = (
            jnp.einsum("tk,ckrz->ctrz", inverse, rows_by_half, precision=lax.Precision.HIGHEST)
            + fixed_by_half
        )
        updated = solved.transpose(1, 0, 2, 3).reshape(total_epochs, share_cells)
        halves = jnp.broadcast_to(solved[None], (src_count // 2,) + solved.shape).reshape(devices, half, size_z)
        mine = lax.all_to_all(halves, ("src", "ep"), split_axis=0, concat_axis=0, tiled=True)
        theirs = lax.ppermute(mine, "src", pairs)
        model_rows = jnp.where(
            core == 0, jnp.concatenate([mine, theirs], axis=1), jnp.concatenate([theirs, mine], axis=1)
        )
    else:
        sent = terms.reshape(devices, share_rows, size_z)
        got = lax.all_to_all(sent, ("src", "ep"), split_axis=0, concat_axis=0, tiled=True)
        solve = np.tile(inverse, (src_count, src_count))
        back = jnp.einsum("pq,qrz->prz", solve, got, precision=lax.Precision.HIGHEST)
        back = back + jnp.tile(fixed_part, (src_count, 1, 1))
        updated = back[:total_epochs].reshape(total_epochs, share_cells)
        model_rows = lax.all_to_all(back, ("src", "ep"), split_axis=0, concat_axis=0, tiled=True)
    shifted = difference(updated) + dual_term
    split_term = shifted - jnp.clip(shifted, -THRESHOLD, THRESHOLD)
    dual_term = shifted - split_term
    model_log = model_rows.reshape(slab_epochs, size_x, size_y, size_z)
    return (model_log, split_term, dual_term)


def solution(mesh):
    return jax.shard_map(
        on_device,
        mesh=mesh,
        in_specs=(
            P("ep", None, None, None),
            P("ep", "src", None, None, None),
            P("ep", "src", None, None, None),
            P("src", None),
            P(),
            P("ep", "src", None),
            P(None, ("src", "ep")),
            P(None, ("src", "ep")),
        ),
        out_specs=(P("ep", None, None, None), P(None, ("src", "ep")), P(None, ("src", "ep"))),
        check_vma=False,
    )
```

```python
import functools

import jax
import jax.numpy as jnp
import numpy as np
from jax import lax
from jax.sharding import PartitionSpec as P
from jax.experimental import pallas as pl
from jax.experimental.pallas import tpu as pltpu

SWEEPS = 4


MASS_TERM = 0.5
RELAXATION = 0.8
CURRENT = 4.0
DATA_WEIGHT = 8.0
STEP_SIZE = 0.5
PENALTY = 64.0
THRESHOLD = 0.1


def pad_side(values, dim_index, at_low):
    widths = [(0, 0)] * values.ndim
    widths[dim_index] = (0, 1) if at_low else (1, 0)
    return jnp.pad(values, widths)


def conductances(conductivity):
    face_weights = []
    diagonal = MASS_TERM * conductivity
    ndims = conductivity.ndim
    for dim_index in range(ndims - 3, ndims):
        length = conductivity.shape[dim_index]
        lower_cells = lax.slice_in_dim(conductivity, 0, length - 1, axis=dim_index)
        upper_cells = lax.slice_in_dim(conductivity, 1, length, axis=dim_index)
        face_weight = 0.5 * (lower_cells + upper_cells)
        face_weights.append(face_weight)
        diagonal = (
            diagonal
            + pad_side(face_weight, dim_index, True)
            + pad_side(face_weight, dim_index, False)
        )
    return (face_weights, diagonal)


def operate(iterate, conductivity, face_weights):
    result = MASS_TERM * conductivity * iterate
    ndims = iterate.ndim
    for position, dim_index in enumerate(range(ndims - 3, ndims)):
        length = iterate.shape[dim_index]
        face_flux = face_weights[position] * (
            lax.slice_in_dim(iterate, 1, length, axis=dim_index)
            - lax.slice_in_dim(iterate, 0, length - 1, axis=dim_index)
        )
        result = (
            result - pad_side(face_flux, dim_index, True) + pad_side(face_flux, dim_index, False)
        )
    return result


def relax(iterate, right_side, conductivity, face_weights, diagonal):
    for sweep_index in range(SWEEPS):
        iterate = (
            iterate
            + RELAXATION * (right_side - operate(iterate, conductivity, face_weights)) / diagonal
        )
    return iterate


def source_field(source_cells, cell_count):
    source_count = source_cells.shape[0]
    row_index = jnp.arange(source_count, dtype=jnp.int32)[:, None] * jnp.ones((1, 2), jnp.int32)
    polarity = jnp.broadcast_to(jnp.array([CURRENT, -CURRENT], jnp.float32), (source_count, 2))
    return (
        jnp.zeros((source_count, cell_count), jnp.float32).at[row_index, source_cells].add(polarity)
    )


def sweep_epoch(model_log, forward, adjoint, sources, receiver_cells, observed):
    grid_shape = forward.shape
    conductivity = jnp.exp(model_log)[None]
    face_weights, diagonal = conductances(conductivity)
    forward = relax(forward, sources.reshape(grid_shape), conductivity, face_weights, diagonal)
    flat_field = forward.reshape(grid_shape[0], -1)
    misfit = flat_field[:, receiver_cells] - observed
    adjoint_source = (
        jnp.zeros_like(flat_field)
        .at[:, receiver_cells]
        .add(DATA_WEIGHT * misfit)
        .reshape(grid_shape)
    )
    adjoint = relax(adjoint, adjoint_source, conductivity, face_weights, diagonal)
    gradient = conductivity[0] * jnp.sum(forward * adjoint, axis=0)
    return (forward, adjoint, gradient)


def temporal_factor(epochs):
    second = (
        jnp.eye(epochs - 2, epochs, dtype=jnp.float32)
        - 2.0 * jnp.eye(epochs - 2, epochs, k=1, dtype=jnp.float32)
        + jnp.eye(epochs - 2, epochs, k=2, dtype=jnp.float32)
    )
    matrix = jnp.eye(epochs, dtype=jnp.float32) + PENALTY * jnp.dot(
        second.T, second, precision=lax.Precision.HIGHEST
    )
    return jnp.linalg.cholesky(matrix)


def difference(values):
    return values[:-2] - 2.0 * values[1:-1] + values[2:]


def difference_adjoint(values):
    widths_low = [(0, 2), (0, 0)]
    widths_mid = [(1, 1), (0, 0)]
    widths_high = [(2, 0), (0, 0)]
    return (
        jnp.pad(values, widths_low)
        - 2.0 * jnp.pad(values, widths_mid)
        + jnp.pad(values, widths_high)
    )


def splitting_update(local_rhs, split_term, dual_term, factor):
    right_side = local_rhs + PENALTY * difference_adjoint(split_term - dual_term)
    updated = jax.scipy.linalg.cho_solve((factor, True), right_side)
    shifted = difference(updated) + dual_term
    split_term = shifted - jnp.clip(shifted, -THRESHOLD, THRESHOLD)
    dual_term = shifted - split_term
    return (updated, split_term, dual_term)


def stencil_kernel(
    size_y,
    half,
    model_ref, forward_ref, adjoint_ref, receiver_vec_ref, observed_vec_ref,
    keep_ref, core_ref, source_ref, receiver_ref,
    *outputs,
):
    drive_ref = outputs[-1]
    rows, lanes = model_ref.shape
    size_x = rows // size_y
    inner = 8
    parts = size_y // inner
    slab_rows = rows // parts
    shape = (parts, size_x, inner, lanes)

    def load(ref):
        slabs = [ref[pl.ds(part, slab_rows, stride=parts), :] for part in range(parts)]
        return jnp.stack(slabs).reshape(shape)

    def store(ref, v):
        for part in range(parts):
            ref[pl.ds(part, slab_rows, stride=parts), :] = v[part].reshape(slab_rows, lanes)

    def next_z(v):
        return pltpu.roll(v, lanes - 1, 3)

    def prev_z(v):
        return pltpu.roll(v, 1, 3)

    def next_y(v):
        return jnp.concatenate([v[1:], pltpu.roll(v[:1], inner - 1, 2)], axis=0)

    def prev_y(v):
        return jnp.concatenate([pltpu.roll(v[parts - 1:], 1, 2), v[:-1]], axis=0)

    def next_x(v):
        return jnp.concatenate([v[:, 1:], v[:, :1]], axis=1)

    def prev_x(v):
        return jnp.concatenate([v[:, size_x - 1:], v[:, : size_x - 1]], axis=1)

    model = load(model_ref)
    conductivity = jnp.exp(model)
    part_id = lax.broadcasted_iota(jnp.int32, shape, 0)
    x_id = lax.broadcasted_iota(jnp.int32, shape, 1)
    y_id = lax.broadcasted_iota(jnp.int32, shape, 2) * parts + part_id
    z_id = lax.broadcasted_iota(jnp.int32, shape, 3)
    zero = jnp.zeros_like(conductivity)
    weight_x = jnp.where(x_id < size_x - 1, 0.5 * (conductivity + next_x(conductivity)), zero)
    weight_y = jnp.where(y_id < size_y - 1, 0.5 * (conductivity + next_y(conductivity)), zero)
    weight_z = jnp.where(z_id < lanes - 1, 0.5 * (conductivity + next_z(conductivity)), zero)
    mass = MASS_TERM * conductivity
    diagonal = mass + weight_x + prev_x(weight_x)
    diagonal = diagonal + weight_y + prev_y(weight_y)
    diagonal = diagonal + weight_z + prev_z(weight_z)

    def operate(v):
        result = mass * v
        flux = weight_x * (next_x(v) - v)
        result = result - flux + prev_x(flux)
        flux = weight_y * (next_y(v) - v)
        result = result - flux + prev_y(flux)
        flux = weight_z * (next_z(v) - v)
        result = result - flux + prev_z(flux)
        return result

    def relax(v, right_side):
        for sweep_index in range(SWEEPS):
            v = v + RELAXATION * (right_side - operate(v)) / diagonal
        return v

    one_row = lax.broadcasted_iota(jnp.int32, (1, lanes), 1)

    def add_at(cell, amount):
        row = cell // lanes
        y = row % size_y
        slot = ((y % parts) * size_x + row // size_y) * inner + y // parts
        drive_ref[pl.ds(slot, 1), :] += jnp.where(one_row == cell % lanes, amount, 0.0)

    drive_ref[...] = jnp.zeros((rows, lanes), jnp.float32)
    add_at(source_ref[0], CURRENT)
    add_at(source_ref[1], -CURRENT)
    forward = relax(load(forward_ref), drive_ref[...].reshape(shape))
    receivers = receiver_ref.shape[0]

    cells = receiver_vec_ref[...]
    slot_id = lax.broadcasted_iota(jnp.int32, (rows, receivers), 0)
    slot_row = ((slot_id // inner) % size_x) * size_y + (slot_id % inner) * parts + slot_id // (size_x * inner)
    placed = (slot_row == cells // lanes).astype(jnp.float32)
    picked = lax.dot_general(
        forward.reshape(rows, lanes), placed, (((0,), (0,)), ((), ())),
        precision=lax.Precision.HIGHEST, preferred_element_type=jnp.float32,
    )
    hit = lax.broadcasted_iota(jnp.int32, (lanes, receivers), 0) == cells % lanes
    value = jnp.sum(jnp.where(hit, picked, 0.0), axis=0, keepdims=True)
    misfit = value - observed_vec_ref[...]
    weighted = jnp.where(hit, DATA_WEIGHT * misfit, 0.0)
    drive = lax.dot_general(
        placed, weighted, (((1,), (1,)), ((), ())),
        precision=lax.Precision.HIGHEST, preferred_element_type=jnp.float32,
    )
    adjoint = relax(load(adjoint_ref), drive.reshape(shape))
    terms = keep_ref[0] * model - STEP_SIZE * (conductivity * (forward * adjoint))
    if not half:
        store(outputs[0], terms)
        return
    keep_out, send_out = outputs[0], outputs[1]
    store(drive_ref, terms)
    core = core_ref[0]
    for chunk in range(keep_out.shape[0]):
        start = chunk * 2 * half
        keep_out[chunk] = drive_ref[pl.ds(pl.multiple_of(start + core * half, half), half), :]
        send_out[chunk] = drive_ref[pl.ds(pl.multiple_of(start + (1 - core) * half, half), half), :]


def stencil_terms(size_y, half, model, forward, adjoint, keep, core, source_cells, receiver_cells, observed):
    rows, lanes = model.shape
    receivers = receiver_cells.shape[0]
    vmem = pl.BlockSpec(memory_space=pltpu.VMEM)
    smem = pl.BlockSpec(memory_space=pltpu.SMEM)
    if half:
        chunks = rows // (2 * half)
        out_shape = (jax.ShapeDtypeStruct((chunks, half, lanes), jnp.float32),) * 2
        out_specs = (vmem, vmem)
    else:
        out_shape = jax.ShapeDtypeStruct((rows, lanes), jnp.float32)
        out_specs = vmem
    return pl.pallas_call(
        functools.partial(stencil_kernel, size_y, half),
        out_shape=out_shape,
        in_specs=[vmem, vmem, vmem, vmem, vmem, smem, smem, smem, smem],
        out_specs=out_specs,
        scratch_shapes=[pltpu.VMEM((rows, lanes), jnp.float32)],
    )(
        model, forward, adjoint, receiver_cells.reshape(1, receivers),
        observed.reshape(1, receivers), keep, core, source_cells, receiver_cells,
    )


def temporal_operators(epochs):
    second = np.eye(epochs - 2, epochs) - 2.0 * np.eye(epochs - 2, epochs, k=1) + np.eye(epochs - 2, epochs, k=2)
    inverse = np.linalg.inv(np.eye(epochs) + PENALTY * second.T @ second)
    coupling = PENALTY * inverse @ second.T
    return inverse.astype(np.float32), coupling.astype(np.float32)


def on_device(
    log_conductivity,
    forward_field,
    adjoint_field,
    source_cells,
    receiver_cells,
    observed,
    split_term,
    dual_term,
):
    slab_epochs, size_x, size_y, size_z = log_conductivity.shape
    cell_count = size_x * size_y * size_z
    src_count = lax.axis_size("src")
    ep_count = lax.axis_size("ep")
    devices = src_count * ep_count
    share_cells = cell_count // devices
    share_rows = share_cells // size_z
    total_epochs = slab_epochs * ep_count
    gaps = split_term.shape[0]
    inverse, coupling = temporal_operators(total_epochs)
    gap = (split_term - dual_term).reshape(gaps, share_rows, size_z)
    fixed_part = jnp.einsum("pk,krz->prz", coupling, gap, precision=lax.Precision.HIGHEST)
    src_index = lax.axis_index("src")
    core = (src_index % 2).astype(jnp.int32)
    pairs = [(i, i ^ 1) for i in range(src_count)]
    half = share_rows // 2 if share_rows % 2 == 0 and src_count % 2 == 0 else 0
    keep = jnp.where((src_index == 0) & (half == 0), 1.0, 0.0).astype(jnp.float32).reshape(1)
    terms = stencil_terms(
        size_y,
        half,
        log_conductivity.reshape(size_x * size_y, size_z),
        forward_field.reshape(size_x * size_y, size_z),
        adjoint_field.reshape(size_x * size_y, size_z),
        keep,
        core.reshape(1),
        source_cells.reshape(2),
        receiver_cells,
        observed.reshape(-1),
    )
    if half:
        kept, sent = terms
        first_chip = jnp.where(src_index < 2, 1.0, 0.0).astype(jnp.float32)
        model_half = lax.dynamic_index_in_dim(
            log_conductivity.reshape(devices, 2, half, size_z), core, axis=1, keepdims=False
        )
        summed = kept + lax.ppermute(sent, "src", pairs) + first_chip * model_half
        got = lax.all_to_all(summed, ("src", "ep"), split_axis=0, concat_axis=0, tiled=True)
        picks = np.kron(np.ones((1, src_count // 2)), np.kron(np.eye(2), inverse)).astype(np.float32)
        fixed_by_half = fixed_part.reshape(total_epochs, 2, half, size_z).transpose(1, 0, 2, 3)
        solved = jnp.einsum("pq,qrz->prz", picks, got, precision=lax.Precision.HIGHEST).reshape(
            2, total_epochs, half, size_z
        ) + fixed_by_half
        updated = solved.transpose(1, 0, 2, 3).reshape(total_epochs, share_cells)
        halves = jnp.broadcast_to(solved[None], (src_count // 2,) + solved.shape).reshape(devices, half, size_z)
        mine = lax.all_to_all(halves, ("src", "ep"), split_axis=0, concat_axis=0, tiled=True)
        theirs = lax.ppermute(mine, "src", pairs)
        model_rows = jnp.where(
            core == 0, jnp.concatenate([mine, theirs], axis=1), jnp.concatenate([theirs, mine], axis=1)
        )
    else:
        sent = terms.reshape(devices, share_rows, size_z)
        got = lax.all_to_all(sent, ("src", "ep"), split_axis=0, concat_axis=0, tiled=True)
        solve = np.tile(inverse, (src_count, src_count))
        back = jnp.einsum("pq,qrz->prz", solve, got, precision=lax.Precision.HIGHEST)
        back = back + jnp.tile(fixed_part, (src_count, 1, 1))
        updated = back[:total_epochs].reshape(total_epochs, share_cells)
        model_rows = lax.all_to_all(back, ("src", "ep"), split_axis=0, concat_axis=0, tiled=True)
    shifted = difference(updated) + dual_term
    split_term = shifted - jnp.clip(shifted, -THRESHOLD, THRESHOLD)
    dual_term = shifted - split_term
    model_log = model_rows.reshape(slab_epochs, size_x, size_y, size_z)
    return (model_log, split_term, dual_term)


def solution(mesh):
    return jax.shard_map(
        on_device,
        mesh=mesh,
        in_specs=(
            P("ep", None, None, None),
            P("ep", "src", None, None, None),
            P("ep", "src", None, None, None),
            P("src", None),
            P(),
            P("ep", "src", None),
            P(None, ("src", "ep")),
            P(None, ("src", "ep")),
        ),
        out_specs=(P("ep", None, None, None), P(None, ("src", "ep")), P(None, ("src", "ep"))),
        check_vma=False,
    )
```

```python
import functools

import jax
import jax.numpy as jnp
import numpy as np
from jax import lax
from jax.sharding import PartitionSpec as P
from jax.experimental import pallas as pl
from jax.experimental.pallas import tpu as pltpu

SWEEPS = 4


MASS_TERM = 0.5
RELAXATION = 0.8
CURRENT = 4.0
DATA_WEIGHT = 8.0
STEP_SIZE = 0.5
PENALTY = 64.0
THRESHOLD = 0.1


def pad_side(values, dim_index, at_low):
    widths = [(0, 0)] * values.ndim
    widths[dim_index] = (0, 1) if at_low else (1, 0)
    return jnp.pad(values, widths)


def conductances(conductivity):
    face_weights = []
    diagonal = MASS_TERM * conductivity
    ndims = conductivity.ndim
    for dim_index in range(ndims - 3, ndims):
        length = conductivity.shape[dim_index]
        lower_cells = lax.slice_in_dim(conductivity, 0, length - 1, axis=dim_index)
        upper_cells = lax.slice_in_dim(conductivity, 1, length, axis=dim_index)
        face_weight = 0.5 * (lower_cells + upper_cells)
        face_weights.append(face_weight)
        diagonal = (
            diagonal
            + pad_side(face_weight, dim_index, True)
            + pad_side(face_weight, dim_index, False)
        )
    return (face_weights, diagonal)


def operate(iterate, conductivity, face_weights):
    result = MASS_TERM * conductivity * iterate
    ndims = iterate.ndim
    for position, dim_index in enumerate(range(ndims - 3, ndims)):
        length = iterate.shape[dim_index]
        face_flux = face_weights[position] * (
            lax.slice_in_dim(iterate, 1, length, axis=dim_index)
            - lax.slice_in_dim(iterate, 0, length - 1, axis=dim_index)
        )
        result = (
            result - pad_side(face_flux, dim_index, True) + pad_side(face_flux, dim_index, False)
        )
    return result


def relax(iterate, right_side, conductivity, face_weights, diagonal):
    for sweep_index in range(SWEEPS):
        iterate = (
            iterate
            + RELAXATION * (right_side - operate(iterate, conductivity, face_weights)) / diagonal
        )
    return iterate


def source_field(source_cells, cell_count):
    source_count = source_cells.shape[0]
    row_index = jnp.arange(source_count, dtype=jnp.int32)[:, None] * jnp.ones((1, 2), jnp.int32)
    polarity = jnp.broadcast_to(jnp.array([CURRENT, -CURRENT], jnp.float32), (source_count, 2))
    return (
        jnp.zeros((source_count, cell_count), jnp.float32).at[row_index, source_cells].add(polarity)
    )


def sweep_epoch(model_log, forward, adjoint, sources, receiver_cells, observed):
    grid_shape = forward.shape
    conductivity = jnp.exp(model_log)[None]
    face_weights, diagonal = conductances(conductivity)
    forward = relax(forward, sources.reshape(grid_shape), conductivity, face_weights, diagonal)
    flat_field = forward.reshape(grid_shape[0], -1)
    misfit = flat_field[:, receiver_cells] - observed
    adjoint_source = (
        jnp.zeros_like(flat_field)
        .at[:, receiver_cells]
        .add(DATA_WEIGHT * misfit)
        .reshape(grid_shape)
    )
    adjoint = relax(adjoint, adjoint_source, conductivity, face_weights, diagonal)
    gradient = conductivity[0] * jnp.sum(forward * adjoint, axis=0)
    return (forward, adjoint, gradient)


def temporal_factor(epochs):
    second = (
        jnp.eye(epochs - 2, epochs, dtype=jnp.float32)
        - 2.0 * jnp.eye(epochs - 2, epochs, k=1, dtype=jnp.float32)
        + jnp.eye(epochs - 2, epochs, k=2, dtype=jnp.float32)
    )
    matrix = jnp.eye(epochs, dtype=jnp.float32) + PENALTY * jnp.dot(
        second.T, second, precision=lax.Precision.HIGHEST
    )
    return jnp.linalg.cholesky(matrix)


def difference(values):
    return values[:-2] - 2.0 * values[1:-1] + values[2:]


def difference_adjoint(values):
    widths_low = [(0, 2), (0, 0)]
    widths_mid = [(1, 1), (0, 0)]
    widths_high = [(2, 0), (0, 0)]
    return (
        jnp.pad(values, widths_low)
        - 2.0 * jnp.pad(values, widths_mid)
        + jnp.pad(values, widths_high)
    )


def splitting_update(local_rhs, split_term, dual_term, factor):
    right_side = local_rhs + PENALTY * difference_adjoint(split_term - dual_term)
    updated = jax.scipy.linalg.cho_solve((factor, True), right_side)
    shifted = difference(updated) + dual_term
    split_term = shifted - jnp.clip(shifted, -THRESHOLD, THRESHOLD)
    dual_term = shifted - split_term
    return (updated, split_term, dual_term)


def stencil_kernel(
    size_y,
    half,
    model_ref, forward_ref, adjoint_ref, receiver_vec_ref, observed_vec_ref,
    keep_ref, core_ref, source_ref, receiver_ref,
    *outputs,
):
    drive_ref = outputs[-1]
    rows, lanes = model_ref.shape
    size_x = rows // size_y
    inner = 8
    parts = size_y // inner
    slab_rows = rows // parts
    shape = (parts, size_x, inner, lanes)

    def load(ref):
        slabs = [ref[pl.ds(part, slab_rows, stride=parts), :] for part in range(parts)]
        return jnp.stack(slabs).reshape(shape)

    def store(ref, v):
        for part in range(parts):
            ref[pl.ds(part, slab_rows, stride=parts), :] = v[part].reshape(slab_rows, lanes)

    def next_z(v):
        return pltpu.roll(v, lanes - 1, 3)

    def prev_z(v):
        return pltpu.roll(v, 1, 3)

    def next_y(v):
        return jnp.concatenate([v[1:], pltpu.roll(v[:1], inner - 1, 2)], axis=0)

    def prev_y(v):
        return jnp.concatenate([pltpu.roll(v[parts - 1:], 1, 2), v[:-1]], axis=0)

    def next_x(v):
        return jnp.concatenate([v[:, 1:], v[:, :1]], axis=1)

    def prev_x(v):
        return jnp.concatenate([v[:, size_x - 1:], v[:, : size_x - 1]], axis=1)

    model = load(model_ref)
    conductivity = jnp.exp(model)
    part_id = lax.broadcasted_iota(jnp.int32, shape, 0)
    x_id = lax.broadcasted_iota(jnp.int32, shape, 1)
    y_id = lax.broadcasted_iota(jnp.int32, shape, 2) * parts + part_id
    z_id = lax.broadcasted_iota(jnp.int32, shape, 3)
    zero = jnp.zeros_like(conductivity)
    weight_x = jnp.where(x_id < size_x - 1, 0.5 * (conductivity + next_x(conductivity)), zero)
    weight_y = jnp.where(y_id < size_y - 1, 0.5 * (conductivity + next_y(conductivity)), zero)
    weight_z = jnp.where(z_id < lanes - 1, 0.5 * (conductivity + next_z(conductivity)), zero)
    mass = MASS_TERM * conductivity
    diagonal = mass + weight_x + prev_x(weight_x)
    diagonal = diagonal + weight_y + prev_y(weight_y)
    diagonal = diagonal + weight_z + prev_z(weight_z)

    def operate(v):
        result = mass * v
        flux = weight_x * (next_x(v) - v)
        result = result - flux + prev_x(flux)
        flux = weight_y * (next_y(v) - v)
        result = result - flux + prev_y(flux)
        flux = weight_z * (next_z(v) - v)
        result = result - flux + prev_z(flux)
        return result

    def relax(v, right_side):
        for sweep_index in range(SWEEPS):
            v = v + RELAXATION * (right_side - operate(v)) / diagonal
        return v

    one_row = lax.broadcasted_iota(jnp.int32, (1, lanes), 1)

    def add_at(cell, amount):
        row = cell // lanes
        y = row % size_y
        slot = ((y % parts) * size_x + row // size_y) * inner + y // parts
        drive_ref[pl.ds(slot, 1), :] += jnp.where(one_row == cell % lanes, amount, 0.0)

    drive_ref[...] = jnp.zeros((rows, lanes), jnp.float32)
    add_at(source_ref[0], CURRENT)
    add_at(source_ref[1], -CURRENT)
    forward = relax(load(forward_ref), drive_ref[...].reshape(shape))
    receivers = receiver_ref.shape[0]

    cells = receiver_vec_ref[...]
    slot_id = lax.broadcasted_iota(jnp.int32, (rows, receivers), 0)
    slot_row = ((slot_id // inner) % size_x) * size_y + (slot_id % inner) * parts + slot_id // (size_x * inner)
    placed = (slot_row == cells // lanes).astype(jnp.float32)
    picked = lax.dot_general(
        forward.reshape(rows, lanes), placed, (((0,), (0,)), ((), ())),
        precision=lax.Precision.HIGH, preferred_element_type=jnp.float32,
    )
    hit = lax.broadcasted_iota(jnp.int32, (lanes, receivers), 0) == cells % lanes
    value = jnp.sum(jnp.where(hit, picked, 0.0), axis=0, keepdims=True)
    misfit = value - observed_vec_ref[...]
    weighted = jnp.where(hit, DATA_WEIGHT * misfit, 0.0)
    drive = lax.dot_general(
        placed, weighted, (((1,), (1,)), ((), ())),
        precision=lax.Precision.HIGH, preferred_element_type=jnp.float32,
    )
    adjoint = relax(load(adjoint_ref), drive.reshape(shape))
    terms = keep_ref[0] * model - STEP_SIZE * (conductivity * (forward * adjoint))
    if not half:
        store(outputs[0], terms)
        return
    keep_out, send_out = outputs[0], outputs[1]
    store(drive_ref, terms)
    core = core_ref[0]
    for chunk in range(keep_out.shape[0]):
        start = chunk * 2 * half
        keep_out[chunk] = drive_ref[pl.ds(pl.multiple_of(start + core * half, half), half), :]
        send_out[chunk] = drive_ref[pl.ds(pl.multiple_of(start + (1 - core) * half, half), half), :]


def stencil_terms(size_y, half, model, forward, adjoint, keep, core, source_cells, receiver_cells, observed):
    rows, lanes = model.shape
    receivers = receiver_cells.shape[0]
    vmem = pl.BlockSpec(memory_space=pltpu.VMEM)
    smem = pl.BlockSpec(memory_space=pltpu.SMEM)
    if half:
        chunks = rows // (2 * half)
        out_shape = (jax.ShapeDtypeStruct((chunks, half, lanes), jnp.float32),) * 2
        out_specs = (vmem, vmem)
    else:
        out_shape = jax.ShapeDtypeStruct((rows, lanes), jnp.float32)
        out_specs = vmem
    return pl.pallas_call(
        functools.partial(stencil_kernel, size_y, half),
        out_shape=out_shape,
        in_specs=[vmem, vmem, vmem, vmem, vmem, smem, smem, smem, smem],
        out_specs=out_specs,
        scratch_shapes=[pltpu.VMEM((rows, lanes), jnp.float32)],
    )(
        model, forward, adjoint, receiver_cells.reshape(1, receivers),
        observed.reshape(1, receivers), keep, core, source_cells, receiver_cells,
    )


def temporal_operators(epochs):
    second = np.eye(epochs - 2, epochs) - 2.0 * np.eye(epochs - 2, epochs, k=1) + np.eye(epochs - 2, epochs, k=2)
    inverse = np.linalg.inv(np.eye(epochs) + PENALTY * second.T @ second)
    coupling = PENALTY * inverse @ second.T
    return inverse.astype(np.float32), coupling.astype(np.float32)


def on_device(
    log_conductivity,
    forward_field,
    adjoint_field,
    source_cells,
    receiver_cells,
    observed,
    split_term,
    dual_term,
):
    slab_epochs, size_x, size_y, size_z = log_conductivity.shape
    cell_count = size_x * size_y * size_z
    src_count = lax.axis_size("src")
    ep_count = lax.axis_size("ep")
    devices = src_count * ep_count
    share_cells = cell_count // devices
    share_rows = share_cells // size_z
    total_epochs = slab_epochs * ep_count
    gaps = split_term.shape[0]
    inverse, coupling = temporal_operators(total_epochs)
    gap = (split_term - dual_term).reshape(gaps, share_rows, size_z)
    fixed_part = jnp.einsum("pk,krz->prz", coupling, gap, precision=lax.Precision.HIGHEST)
    src_index = lax.axis_index("src")
    core = (src_index % 2).astype(jnp.int32)
    pairs = [(i, i ^ 1) for i in range(src_count)]
    half = share_rows // 2 if share_rows % 2 == 0 and src_count % 2 == 0 else 0
    keep = jnp.where((src_index == 0) & (half == 0), 1.0, 0.0).astype(jnp.float32).reshape(1)
    terms = stencil_terms(
        size_y,
        half,
        log_conductivity.reshape(size_x * size_y, size_z),
        forward_field.reshape(size_x * size_y, size_z),
        adjoint_field.reshape(size_x * size_y, size_z),
        keep,
        core.reshape(1),
        source_cells.reshape(2),
        receiver_cells,
        observed.reshape(-1),
    )
    if half:
        kept, sent = terms
        first_chip = jnp.where(src_index < 2, 1.0, 0.0).astype(jnp.float32)
        model_half = lax.dynamic_index_in_dim(
            log_conductivity.reshape(devices, 2, half, size_z), core, axis=1, keepdims=False
        )
        summed = kept + lax.ppermute(sent, "src", pairs) + first_chip * model_half
        got = lax.all_to_all(summed, ("src", "ep"), split_axis=0, concat_axis=0, tiled=True)
        picks = np.kron(np.ones((1, src_count // 2)), np.kron(np.eye(2), inverse)).astype(np.float32)
        fixed_by_half = fixed_part.reshape(total_epochs, 2, half, size_z).transpose(1, 0, 2, 3)
        solved = jnp.einsum("pq,qrz->prz", picks, got, precision=lax.Precision.HIGH).reshape(
            2, total_epochs, half, size_z
        ) + fixed_by_half
        updated = solved.transpose(1, 0, 2, 3).reshape(total_epochs, share_cells)
        halves = jnp.broadcast_to(solved[None], (src_count // 2,) + solved.shape).reshape(devices, half, size_z)
        mine = lax.all_to_all(halves, ("src", "ep"), split_axis=0, concat_axis=0, tiled=True)
        theirs = lax.ppermute(mine, "src", pairs)
        model_rows = jnp.where(
            core == 0, jnp.concatenate([mine, theirs], axis=1), jnp.concatenate([theirs, mine], axis=1)
        )
    else:
        sent = terms.reshape(devices, share_rows, size_z)
        got = lax.all_to_all(sent, ("src", "ep"), split_axis=0, concat_axis=0, tiled=True)
        solve = np.tile(inverse, (src_count, src_count))
        back = jnp.einsum("pq,qrz->prz", solve, got, precision=lax.Precision.HIGHEST)
        back = back + jnp.tile(fixed_part, (src_count, 1, 1))
        updated = back[:total_epochs].reshape(total_epochs, share_cells)
        model_rows = lax.all_to_all(back, ("src", "ep"), split_axis=0, concat_axis=0, tiled=True)
    shifted = difference(updated) + dual_term
    split_term = shifted - jnp.clip(shifted, -THRESHOLD, THRESHOLD)
    dual_term = shifted - split_term
    model_log = model_rows.reshape(slab_epochs, size_x, size_y, size_z)
    return (model_log, split_term, dual_term)


def solution(mesh):
    return jax.shard_map(
        on_device,
        mesh=mesh,
        in_specs=(
            P("ep", None, None, None),
            P("ep", "src", None, None, None),
            P("ep", "src", None, None, None),
            P("src", None),
            P(),
            P("ep", "src", None),
            P(None, ("src", "ep")),
            P(None, ("src", "ep")),
        ),
        out_specs=(P("ep", None, None, None), P(None, ("src", "ep")), P(None, ("src", "ep"))),
        check_vma=False,
    )
```

```python
import functools

import jax
import jax.numpy as jnp
import numpy as np
from jax import lax
from jax.sharding import PartitionSpec as P
from jax.experimental import pallas as pl
from jax.experimental.pallas import tpu as pltpu

SWEEPS = 4


MASS_TERM = 0.5
RELAXATION = 0.8
CURRENT = 4.0
DATA_WEIGHT = 8.0
STEP_SIZE = 0.5
PENALTY = 64.0
THRESHOLD = 0.1


def pad_side(values, dim_index, at_low):
    widths = [(0, 0)] * values.ndim
    widths[dim_index] = (0, 1) if at_low else (1, 0)
    return jnp.pad(values, widths)


def conductances(conductivity):
    face_weights = []
    diagonal = MASS_TERM * conductivity
    ndims = conductivity.ndim
    for dim_index in range(ndims - 3, ndims):
        length = conductivity.shape[dim_index]
        lower_cells = lax.slice_in_dim(conductivity, 0, length - 1, axis=dim_index)
        upper_cells = lax.slice_in_dim(conductivity, 1, length, axis=dim_index)
        face_weight = 0.5 * (lower_cells + upper_cells)
        face_weights.append(face_weight)
        diagonal = (
            diagonal
            + pad_side(face_weight, dim_index, True)
            + pad_side(face_weight, dim_index, False)
        )
    return (face_weights, diagonal)


def operate(iterate, conductivity, face_weights):
    result = MASS_TERM * conductivity * iterate
    ndims = iterate.ndim
    for position, dim_index in enumerate(range(ndims - 3, ndims)):
        length = iterate.shape[dim_index]
        face_flux = face_weights[position] * (
            lax.slice_in_dim(iterate, 1, length, axis=dim_index)
            - lax.slice_in_dim(iterate, 0, length - 1, axis=dim_index)
        )
        result = (
            result - pad_side(face_flux, dim_index, True) + pad_side(face_flux, dim_index, False)
        )
    return result


def relax(iterate, right_side, conductivity, face_weights, diagonal):
    for sweep_index in range(SWEEPS):
        iterate = (
            iterate
            + RELAXATION * (right_side - operate(iterate, conductivity, face_weights)) / diagonal
        )
    return iterate


def source_field(source_cells, cell_count):
    source_count = source_cells.shape[0]
    row_index = jnp.arange(source_count, dtype=jnp.int32)[:, None] * jnp.ones((1, 2), jnp.int32)
    polarity = jnp.broadcast_to(jnp.array([CURRENT, -CURRENT], jnp.float32), (source_count, 2))
    return (
        jnp.zeros((source_count, cell_count), jnp.float32).at[row_index, source_cells].add(polarity)
    )


def sweep_epoch(model_log, forward, adjoint, sources, receiver_cells, observed):
    grid_shape = forward.shape
    conductivity = jnp.exp(model_log)[None]
    face_weights, diagonal = conductances(conductivity)
    forward = relax(forward, sources.reshape(grid_shape), conductivity, face_weights, diagonal)
    flat_field = forward.reshape(grid_shape[0], -1)
    misfit = flat_field[:, receiver_cells] - observed
    adjoint_source = (
        jnp.zeros_like(flat_field)
        .at[:, receiver_cells]
        .add(DATA_WEIGHT * misfit)
        .reshape(grid_shape)
    )
    adjoint = relax(adjoint, adjoint_source, conductivity, face_weights, diagonal)
    gradient = conductivity[0] * jnp.sum(forward * adjoint, axis=0)
    return (forward, adjoint, gradient)


def temporal_factor(epochs):
    second = (
        jnp.eye(epochs - 2, epochs, dtype=jnp.float32)
        - 2.0 * jnp.eye(epochs - 2, epochs, k=1, dtype=jnp.float32)
        + jnp.eye(epochs - 2, epochs, k=2, dtype=jnp.float32)
    )
    matrix = jnp.eye(epochs, dtype=jnp.float32) + PENALTY * jnp.dot(
        second.T, second, precision=lax.Precision.HIGHEST
    )
    return jnp.linalg.cholesky(matrix)


def difference(values):
    return values[:-2] - 2.0 * values[1:-1] + values[2:]


def difference_adjoint(values):
    widths_low = [(0, 2), (0, 0)]
    widths_mid = [(1, 1), (0, 0)]
    widths_high = [(2, 0), (0, 0)]
    return (
        jnp.pad(values, widths_low)
        - 2.0 * jnp.pad(values, widths_mid)
        + jnp.pad(values, widths_high)
    )


def splitting_update(local_rhs, split_term, dual_term, factor):
    right_side = local_rhs + PENALTY * difference_adjoint(split_term - dual_term)
    updated = jax.scipy.linalg.cho_solve((factor, True), right_side)
    shifted = difference(updated) + dual_term
    split_term = shifted - jnp.clip(shifted, -THRESHOLD, THRESHOLD)
    dual_term = shifted - split_term
    return (updated, split_term, dual_term)


def stencil_kernel(
    size_y,
    half,
    model_ref, forward_ref, adjoint_ref, receiver_vec_ref, observed_vec_ref,
    keep_ref, core_ref, source_ref, receiver_ref,
    *outputs,
):
    drive_ref = outputs[-1]
    rows, lanes = model_ref.shape
    size_x = rows // size_y
    inner = 8
    parts = size_y // inner
    slab_rows = rows // parts
    shape = (parts, size_x, inner, lanes)

    def load(ref):
        slabs = [ref[pl.ds(part, slab_rows, stride=parts), :] for part in range(parts)]
        return jnp.stack(slabs).reshape(shape)

    def store(ref, v):
        for part in range(parts):
            ref[pl.ds(part, slab_rows, stride=parts), :] = v[part].reshape(slab_rows, lanes)

    def next_z(v):
        return pltpu.roll(v, lanes - 1, 3)

    def prev_z(v):
        return pltpu.roll(v, 1, 3)

    def next_y(v):
        return jnp.concatenate([v[1:], pltpu.roll(v[:1], inner - 1, 2)], axis=0)

    def prev_y(v):
        return jnp.concatenate([pltpu.roll(v[parts - 1:], 1, 2), v[:-1]], axis=0)

    def next_x(v):
        return jnp.concatenate([v[:, 1:], v[:, :1]], axis=1)

    def prev_x(v):
        return jnp.concatenate([v[:, size_x - 1:], v[:, : size_x - 1]], axis=1)

    model = load(model_ref)
    conductivity = jnp.exp(model)
    part_id = lax.broadcasted_iota(jnp.int32, shape, 0)
    x_id = lax.broadcasted_iota(jnp.int32, shape, 1)
    y_id = lax.broadcasted_iota(jnp.int32, shape, 2) * parts + part_id
    z_id = lax.broadcasted_iota(jnp.int32, shape, 3)
    zero = jnp.zeros_like(conductivity)
    weight_x = jnp.where(x_id < size_x - 1, 0.5 * (conductivity + next_x(conductivity)), zero)
    weight_y = jnp.where(y_id < size_y - 1, 0.5 * (conductivity + next_y(conductivity)), zero)
    weight_z = jnp.where(z_id < lanes - 1, 0.5 * (conductivity + next_z(conductivity)), zero)
    mass = MASS_TERM * conductivity
    diagonal = mass + weight_x + prev_x(weight_x)
    diagonal = diagonal + weight_y + prev_y(weight_y)
    diagonal = diagonal + weight_z + prev_z(weight_z)

    def operate(v):
        result = mass * v
        flux = weight_x * (next_x(v) - v)
        result = result - flux + prev_x(flux)
        flux = weight_y * (next_y(v) - v)
        result = result - flux + prev_y(flux)
        flux = weight_z * (next_z(v) - v)
        result = result - flux + prev_z(flux)
        return result

    def relax(v, right_side):
        for sweep_index in range(SWEEPS):
            v = v + RELAXATION * (right_side - operate(v)) / diagonal
        return v

    one_row = lax.broadcasted_iota(jnp.int32, (1, lanes), 1)

    def add_at(cell, amount):
        row = cell // lanes
        y = row % size_y
        slot = ((y % parts) * size_x + row // size_y) * inner + y // parts
        drive_ref[pl.ds(slot, 1), :] += jnp.where(one_row == cell % lanes, amount, 0.0)

    drive_ref[...] = jnp.zeros((rows, lanes), jnp.float32)
    add_at(source_ref[0], CURRENT)
    add_at(source_ref[1], -CURRENT)
    forward = relax(load(forward_ref), drive_ref[...].reshape(shape))
    receivers = receiver_ref.shape[0]

    cells = receiver_vec_ref[...]
    slot_id = lax.broadcasted_iota(jnp.int32, (rows, receivers), 0)
    slot_row = ((slot_id // inner) % size_x) * size_y + (slot_id % inner) * parts + slot_id // (size_x * inner)
    placed = (slot_row == cells // lanes).astype(jnp.float32)
    picked = lax.dot_general(
        forward.reshape(rows, lanes), placed, (((0,), (0,)), ((), ())),
        precision=lax.Precision.HIGHEST, preferred_element_type=jnp.float32,
    )
    hit = lax.broadcasted_iota(jnp.int32, (lanes, receivers), 0) == cells % lanes
    value = jnp.sum(jnp.where(hit, picked, 0.0), axis=0, keepdims=True)
    misfit = value - observed_vec_ref[...]
    weighted = jnp.where(hit, DATA_WEIGHT * misfit, 0.0)
    drive = lax.dot_general(
        placed, weighted, (((1,), (1,)), ((), ())),
        precision=lax.Precision.HIGHEST, preferred_element_type=jnp.float32,
    )
    adjoint = relax(load(adjoint_ref), drive.reshape(shape))
    terms = keep_ref[0] * model - STEP_SIZE * (conductivity * (forward * adjoint))
    if not half:
        store(outputs[0], terms)
        return
    keep_out, send_out = outputs[0], outputs[1]
    store(drive_ref, terms)
    core = core_ref[0]
    for chunk in range(keep_out.shape[0]):
        start = chunk * 2 * half
        keep_out[chunk] = drive_ref[pl.ds(pl.multiple_of(start + core * half, half), half), :]
        send_out[chunk] = drive_ref[pl.ds(pl.multiple_of(start + (1 - core) * half, half), half), :]


def stencil_terms(size_y, half, model, forward, adjoint, keep, core, source_cells, receiver_cells, observed):
    rows, lanes = model.shape
    receivers = receiver_cells.shape[0]
    vmem = pl.BlockSpec(memory_space=pltpu.VMEM)
    smem = pl.BlockSpec(memory_space=pltpu.SMEM)
    if half:
        chunks = rows // (2 * half)
        out_shape = (jax.ShapeDtypeStruct((chunks, half, lanes), jnp.float32),) * 2
        out_specs = (vmem, vmem)
    else:
        out_shape = jax.ShapeDtypeStruct((rows, lanes), jnp.float32)
        out_specs = vmem
    return pl.pallas_call(
        functools.partial(stencil_kernel, size_y, half),
        out_shape=out_shape,
        in_specs=[vmem, vmem, vmem, vmem, vmem, smem, smem, smem, smem],
        out_specs=out_specs,
        scratch_shapes=[pltpu.VMEM((rows, lanes), jnp.float32)],
    )(
        model, forward, adjoint, receiver_cells.reshape(1, receivers),
        observed.reshape(1, receivers), keep, core, source_cells, receiver_cells,
    )


def temporal_operators(epochs):
    second = np.eye(epochs - 2, epochs) - 2.0 * np.eye(epochs - 2, epochs, k=1) + np.eye(epochs - 2, epochs, k=2)
    inverse = np.linalg.inv(np.eye(epochs) + PENALTY * second.T @ second)
    coupling = PENALTY * inverse @ second.T
    return inverse.astype(np.float32), coupling.astype(np.float32)


def on_device(
    log_conductivity,
    forward_field,
    adjoint_field,
    source_cells,
    receiver_cells,
    observed,
    split_term,
    dual_term,
):
    slab_epochs, size_x, size_y, size_z = log_conductivity.shape
    cell_count = size_x * size_y * size_z
    src_count = lax.axis_size("src")
    ep_count = lax.axis_size("ep")
    devices = src_count * ep_count
    share_cells = cell_count // devices
    share_rows = share_cells // size_z
    total_epochs = slab_epochs * ep_count
    gaps = split_term.shape[0]
    inverse, coupling = temporal_operators(total_epochs)
    gap = (split_term - dual_term).reshape(gaps, share_rows, size_z)
    fixed_part = jnp.einsum("pk,krz->prz", coupling, gap, precision=lax.Precision.HIGHEST)
    src_index = lax.axis_index("src")
    core = (src_index % 2).astype(jnp.int32)
    pairs = [(i, i ^ 1) for i in range(src_count)]
    half = share_rows // 2 if share_rows % 2 == 0 and src_count % 2 == 0 else 0
    keep = jnp.where((src_index == 0) & (half == 0), 1.0, 0.0).astype(jnp.float32).reshape(1)
    terms = stencil_terms(
        size_y,
        half,
        log_conductivity.reshape(size_x * size_y, size_z),
        forward_field.reshape(size_x * size_y, size_z),
        adjoint_field.reshape(size_x * size_y, size_z),
        keep,
        core.reshape(1),
        source_cells.reshape(2),
        receiver_cells,
        observed.reshape(-1),
    )
    if half:
        kept, sent = terms
        first_chip = jnp.where(src_index < 2, 1.0, 0.0).astype(jnp.float32)
        model_half = lax.dynamic_index_in_dim(
            log_conductivity.reshape(devices, 2, half, size_z), core, axis=1, keepdims=False
        )
        summed = kept + lax.ppermute(sent, "src", pairs) + first_chip * model_half
        got = lax.all_to_all(summed, ("src", "ep"), split_axis=0, concat_axis=0, tiled=True)
        fixed_by_half = fixed_part.reshape(total_epochs, 2, half, size_z).transpose(1, 0, 2, 3)
        by_chip = got.reshape(src_count // 2, 2, total_epochs, half, size_z)
        rows_by_half = by_chip[0]
        for chip in range(1, src_count // 2):
            rows_by_half = rows_by_half + by_chip[chip]
        solved_rows = []
        for t in range(total_epochs):
            total = fixed_by_half[:, t]
            for k in range(total_epochs):
                total = total + float(inverse[t, k]) * rows_by_half[:, k]
            solved_rows.append(total)
        solved = jnp.stack(solved_rows, axis=1)
        updated = solved.transpose(1, 0, 2, 3).reshape(total_epochs, share_cells)
        halves = jnp.concatenate([solved] * (src_count // 2), axis=0).reshape(devices, half, size_z)
        mine = lax.all_to_all(halves, ("src", "ep"), split_axis=0, concat_axis=0, tiled=True)
        theirs = lax.ppermute(mine, "src", pairs)
        model_rows = jnp.where(
            core == 0, jnp.concatenate([mine, theirs], axis=1), jnp.concatenate([theirs, mine], axis=1)
        )
    else:
        sent = terms.reshape(devices, share_rows, size_z)
        got = lax.all_to_all(sent, ("src", "ep"), split_axis=0, concat_axis=0, tiled=True)
        solve = np.tile(inverse, (src_count, src_count))
        back = jnp.einsum("pq,qrz->prz", solve, got, precision=lax.Precision.HIGHEST)
        back = back + jnp.tile(fixed_part, (src_count, 1, 1))
        updated = back[:total_epochs].reshape(total_epochs, share_cells)
        model_rows = lax.all_to_all(back, ("src", "ep"), split_axis=0, concat_axis=0, tiled=True)
    shifted = difference(updated) + dual_term
    split_term = shifted - jnp.clip(shifted, -THRESHOLD, THRESHOLD)
    dual_term = shifted - split_term
    model_log = model_rows.reshape(slab_epochs, size_x, size_y, size_z)
    return (model_log, split_term, dual_term)


def solution(mesh):
    return jax.shard_map(
        on_device,
        mesh=mesh,
        in_specs=(
            P("ep", None, None, None),
            P("ep", "src", None, None, None),
            P("ep", "src", None, None, None),
            P("src", None),
            P(),
            P("ep", "src", None),
            P(None, ("src", "ep")),
            P(None, ("src", "ep")),
        ),
        out_specs=(P("ep", None, None, None), P(None, ("src", "ep")), P(None, ("src", "ep"))),
        check_vma=False,
    )
```

```python
import functools

import jax
import jax.numpy as jnp
import numpy as np
from jax import lax
from jax.sharding import PartitionSpec as P
from jax.experimental import pallas as pl
from jax.experimental.pallas import tpu as pltpu

SWEEPS = 4


MASS_TERM = 0.5
RELAXATION = 0.8
CURRENT = 4.0
DATA_WEIGHT = 8.0
STEP_SIZE = 0.5
PENALTY = 64.0
THRESHOLD = 0.1


def pad_side(values, dim_index, at_low):
    widths = [(0, 0)] * values.ndim
    widths[dim_index] = (0, 1) if at_low else (1, 0)
    return jnp.pad(values, widths)


def conductances(conductivity):
    face_weights = []
    diagonal = MASS_TERM * conductivity
    ndims = conductivity.ndim
    for dim_index in range(ndims - 3, ndims):
        length = conductivity.shape[dim_index]
        lower_cells = lax.slice_in_dim(conductivity, 0, length - 1, axis=dim_index)
        upper_cells = lax.slice_in_dim(conductivity, 1, length, axis=dim_index)
        face_weight = 0.5 * (lower_cells + upper_cells)
        face_weights.append(face_weight)
        diagonal = (
            diagonal
            + pad_side(face_weight, dim_index, True)
            + pad_side(face_weight, dim_index, False)
        )
    return (face_weights, diagonal)


def operate(iterate, conductivity, face_weights):
    result = MASS_TERM * conductivity * iterate
    ndims = iterate.ndim
    for position, dim_index in enumerate(range(ndims - 3, ndims)):
        length = iterate.shape[dim_index]
        face_flux = face_weights[position] * (
            lax.slice_in_dim(iterate, 1, length, axis=dim_index)
            - lax.slice_in_dim(iterate, 0, length - 1, axis=dim_index)
        )
        result = (
            result - pad_side(face_flux, dim_index, True) + pad_side(face_flux, dim_index, False)
        )
    return result


def relax(iterate, right_side, conductivity, face_weights, diagonal):
    for sweep_index in range(SWEEPS):
        iterate = (
            iterate
            + RELAXATION * (right_side - operate(iterate, conductivity, face_weights)) / diagonal
        )
    return iterate


def source_field(source_cells, cell_count):
    source_count = source_cells.shape[0]
    row_index = jnp.arange(source_count, dtype=jnp.int32)[:, None] * jnp.ones((1, 2), jnp.int32)
    polarity = jnp.broadcast_to(jnp.array([CURRENT, -CURRENT], jnp.float32), (source_count, 2))
    return (
        jnp.zeros((source_count, cell_count), jnp.float32).at[row_index, source_cells].add(polarity)
    )


def sweep_epoch(model_log, forward, adjoint, sources, receiver_cells, observed):
    grid_shape = forward.shape
    conductivity = jnp.exp(model_log)[None]
    face_weights, diagonal = conductances(conductivity)
    forward = relax(forward, sources.reshape(grid_shape), conductivity, face_weights, diagonal)
    flat_field = forward.reshape(grid_shape[0], -1)
    misfit = flat_field[:, receiver_cells] - observed
    adjoint_source = (
        jnp.zeros_like(flat_field)
        .at[:, receiver_cells]
        .add(DATA_WEIGHT * misfit)
        .reshape(grid_shape)
    )
    adjoint = relax(adjoint, adjoint_source, conductivity, face_weights, diagonal)
    gradient = conductivity[0] * jnp.sum(forward * adjoint, axis=0)
    return (forward, adjoint, gradient)


def temporal_factor(epochs):
    second = (
        jnp.eye(epochs - 2, epochs, dtype=jnp.float32)
        - 2.0 * jnp.eye(epochs - 2, epochs, k=1, dtype=jnp.float32)
        + jnp.eye(epochs - 2, epochs, k=2, dtype=jnp.float32)
    )
    matrix = jnp.eye(epochs, dtype=jnp.float32) + PENALTY * jnp.dot(
        second.T, second, precision=lax.Precision.HIGHEST
    )
    return jnp.linalg.cholesky(matrix)


def difference(values):
    return values[:-2] - 2.0 * values[1:-1] + values[2:]


def difference_adjoint(values):
    widths_low = [(0, 2), (0, 0)]
    widths_mid = [(1, 1), (0, 0)]
    widths_high = [(2, 0), (0, 0)]
    return (
        jnp.pad(values, widths_low)
        - 2.0 * jnp.pad(values, widths_mid)
        + jnp.pad(values, widths_high)
    )


def splitting_update(local_rhs, split_term, dual_term, factor):
    right_side = local_rhs + PENALTY * difference_adjoint(split_term - dual_term)
    updated = jax.scipy.linalg.cho_solve((factor, True), right_side)
    shifted = difference(updated) + dual_term
    split_term = shifted - jnp.clip(shifted, -THRESHOLD, THRESHOLD)
    dual_term = shifted - split_term
    return (updated, split_term, dual_term)


def stencil_kernel(
    size_y,
    model_ref, forward_ref, adjoint_ref, receiver_vec_ref, observed_vec_ref,
    keep_ref, source_ref, receiver_ref,
    out_ref, drive_ref,
):
    rows, lanes = model_ref.shape
    size_x = rows // size_y
    inner = 8
    parts = size_y // inner
    slab_rows = rows // parts
    shape = (parts, size_x, inner, lanes)

    def load(ref):
        slabs = [ref[pl.ds(part, slab_rows, stride=parts), :] for part in range(parts)]
        return jnp.stack(slabs).reshape(shape)

    def store(ref, v):
        for part in range(parts):
            ref[pl.ds(part, slab_rows, stride=parts), :] = v[part].reshape(slab_rows, lanes)

    def next_z(v):
        return pltpu.roll(v, lanes - 1, 3)

    def prev_z(v):
        return pltpu.roll(v, 1, 3)

    def next_y(v):
        return jnp.concatenate([v[1:], pltpu.roll(v[:1], inner - 1, 2)], axis=0)

    def prev_y(v):
        return jnp.concatenate([pltpu.roll(v[parts - 1:], 1, 2), v[:-1]], axis=0)

    def next_x(v):
        return jnp.concatenate([v[:, 1:], v[:, :1]], axis=1)

    def prev_x(v):
        return jnp.concatenate([v[:, size_x - 1:], v[:, : size_x - 1]], axis=1)

    model = load(model_ref)
    conductivity = jnp.exp(model)
    part_id = lax.broadcasted_iota(jnp.int32, shape, 0)
    x_id = lax.broadcasted_iota(jnp.int32, shape, 1)
    y_id = lax.broadcasted_iota(jnp.int32, shape, 2) * parts + part_id
    z_id = lax.broadcasted_iota(jnp.int32, shape, 3)
    zero = jnp.zeros_like(conductivity)
    weight_x = jnp.where(x_id < size_x - 1, 0.5 * (conductivity + next_x(conductivity)), zero)
    weight_y = jnp.where(y_id < size_y - 1, 0.5 * (conductivity + next_y(conductivity)), zero)
    weight_z = jnp.where(z_id < lanes - 1, 0.5 * (conductivity + next_z(conductivity)), zero)
    mass = MASS_TERM * conductivity
    diagonal = mass + weight_x + prev_x(weight_x)
    diagonal = diagonal + weight_y + prev_y(weight_y)
    diagonal = diagonal + weight_z + prev_z(weight_z)

    def operate(v):
        result = mass * v
        flux = weight_x * (next_x(v) - v)
        result = result - flux + prev_x(flux)
        flux = weight_y * (next_y(v) - v)
        result = result - flux + prev_y(flux)
        flux = weight_z * (next_z(v) - v)
        result = result - flux + prev_z(flux)
        return result

    def relax(v, right_side):
        for sweep_index in range(SWEEPS):
            v = v + RELAXATION * (right_side - operate(v)) / diagonal
        return v

    one_row = lax.broadcasted_iota(jnp.int32, (1, lanes), 1)

    def add_at(cell, amount):
        row = cell // lanes
        y = row % size_y
        slot = ((y % parts) * size_x + row // size_y) * inner + y // parts
        drive_ref[pl.ds(slot, 1), :] += jnp.where(one_row == cell % lanes, amount, 0.0)

    drive_ref[...] = jnp.zeros((rows, lanes), jnp.float32)
    add_at(source_ref[0], CURRENT)
    add_at(source_ref[1], -CURRENT)
    forward = relax(load(forward_ref), drive_ref[...].reshape(shape))
    receivers = receiver_ref.shape[0]

    cells = receiver_vec_ref[...]
    slot_id = lax.broadcasted_iota(jnp.int32, (rows, receivers), 0)
    slot_row = ((slot_id // inner) % size_x) * size_y + (slot_id % inner) * parts + slot_id // (size_x * inner)
    placed = (slot_row == cells // lanes).astype(jnp.float32)
    picked = lax.dot_general(
        forward.reshape(rows, lanes), placed, (((0,), (0,)), ((), ())),
        precision=lax.Precision.HIGHEST, preferred_element_type=jnp.float32,
    )
    hit = lax.broadcasted_iota(jnp.int32, (lanes, receivers), 0) == cells % lanes
    value = jnp.sum(jnp.where(hit, picked, 0.0), axis=0, keepdims=True)
    misfit = value - observed_vec_ref[...]
    weighted = jnp.where(hit, DATA_WEIGHT * misfit, 0.0)
    drive = lax.dot_general(
        placed, weighted, (((1,), (1,)), ((), ())),
        precision=lax.Precision.HIGHEST, preferred_element_type=jnp.float32,
    )
    adjoint = relax(load(adjoint_ref), drive.reshape(shape))
    store(out_ref, keep_ref[0] * model - STEP_SIZE * (conductivity * (forward * adjoint)))


def stencil_terms(size_y, model, forward, adjoint, keep, source_cells, receiver_cells, observed):
    rows, lanes = model.shape
    receivers = receiver_cells.shape[0]
    vmem = pl.BlockSpec(memory_space=pltpu.VMEM)
    smem = pl.BlockSpec(memory_space=pltpu.SMEM)
    return pl.pallas_call(
        functools.partial(stencil_kernel, size_y),
        out_shape=jax.ShapeDtypeStruct((rows, lanes), jnp.float32),
        in_specs=[vmem, vmem, vmem, vmem, vmem, smem, smem, smem],
        out_specs=vmem,
        scratch_shapes=[pltpu.VMEM((rows, lanes), jnp.float32)],
    )(
        model, forward, adjoint, receiver_cells.reshape(1, receivers),
        observed.reshape(1, receivers), keep, source_cells, receiver_cells,
    )


def temporal_operators(epochs, src_count):
    second = np.eye(epochs - 2, epochs) - 2.0 * np.eye(epochs - 2, epochs, k=1) + np.eye(epochs - 2, epochs, k=2)
    inverse = np.linalg.inv(np.eye(epochs) + PENALTY * second.T @ second)
    solve = np.tile(inverse, (src_count, src_count))
    coupling = np.tile(PENALTY * inverse @ second.T, (src_count, 1))
    return solve.astype(np.float32), jnp.asarray(coupling, jnp.float32)


def on_device(
    log_conductivity,
    forward_field,
    adjoint_field,
    source_cells,
    receiver_cells,
    observed,
    split_term,
    dual_term,
):
    slab_epochs, size_x, size_y, size_z = log_conductivity.shape
    cell_count = size_x * size_y * size_z
    src_count = lax.axis_size("src")
    ep_count = lax.axis_size("ep")
    devices = src_count * ep_count
    share_cells = cell_count // devices
    share_rows = share_cells // size_z
    total_epochs = slab_epochs * ep_count
    keep = jnp.where(lax.axis_index("src") == 0, 1.0, 0.0).astype(jnp.float32).reshape(1)
    partial_rhs = stencil_terms(
        size_y,
        log_conductivity.reshape(size_x * size_y, size_z),
        forward_field.reshape(size_x * size_y, size_z),
        adjoint_field.reshape(size_x * size_y, size_z),
        keep,
        source_cells.reshape(2),
        receiver_cells,
        observed.reshape(-1),
    )
    sent = partial_rhs.reshape(devices, share_rows, size_z)
    got = lax.all_to_all(sent, ("src", "ep"), split_axis=0, concat_axis=0, tiled=True)
    solve, coupling = temporal_operators(total_epochs, src_count)
    gaps = split_term.shape[0]
    gap = (split_term - dual_term).reshape(gaps, share_rows, size_z)
    fixed_part = jnp.einsum("pk,krz->prz", coupling, gap, precision=lax.Precision.HIGHEST)
    half = share_rows // 2
    if share_rows % 2 == 0 and src_count % 2 == 0:
        inverse = np.asarray(solve[:total_epochs, :total_epochs], np.float64)
        summed = got[:total_epochs]
        for s in range(1, src_count):
            summed = summed + got[s * total_epochs : (s + 1) * total_epochs]
        solved_rows = []
        for t in range(total_epochs):
            total = fixed_part[t]
            for k in range(total_epochs):
                total = total + float(inverse[t, k]) * summed[k]
            solved_rows.append(total)
        solved = jnp.stack(solved_rows)
        updated = solved.reshape(total_epochs, share_cells)
        core = lax.axis_index("src") % 2
        own_rows = solved.reshape(total_epochs, 2, half, size_z).transpose(1, 0, 2, 3)
        halves = jnp.concatenate([own_rows] * (src_count // 2), axis=0).reshape(devices, half, size_z)
        mine = lax.all_to_all(halves, ("src", "ep"), split_axis=0, concat_axis=0, tiled=True)
        theirs = lax.ppermute(mine, "src", [(i, i ^ 1) for i in range(src_count)])
        model_rows = jnp.where(
            core == 0, jnp.concatenate([mine, theirs], axis=1), jnp.concatenate([theirs, mine], axis=1)
        )
    else:
        back = jnp.einsum("pq,qrz->prz", solve, got, precision=lax.Precision.HIGHEST) + fixed_part
        updated = back[:total_epochs].reshape(total_epochs, share_cells)
        model_rows = lax.all_to_all(back, ("src", "ep"), split_axis=0, concat_axis=0, tiled=True)
    shifted = difference(updated) + dual_term
    split_term = shifted - jnp.clip(shifted, -THRESHOLD, THRESHOLD)
    dual_term = shifted - split_term
    model_log = model_rows.reshape(slab_epochs, size_x, size_y, size_z)
    return (model_log, split_term, dual_term)


def solution(mesh):
    return jax.shard_map(
        on_device,
        mesh=mesh,
        in_specs=(
            P("ep", None, None, None),
            P("ep", "src", None, None, None),
            P("ep", "src", None, None, None),
            P("src", None),
            P(),
            P("ep", "src", None),
            P(None, ("src", "ep")),
            P(None, ("src", "ep")),
        ),
        out_specs=(P("ep", None, None, None), P(None, ("src", "ep")), P(None, ("src", "ep"))),
        check_vma=False,
    )
```
